128 devices in a mesh: req: 16 (over y, x), head: 8 (over z, core).
Axes of the slice: x: 4, y: 4, z: 4, core: 2. Of those that a mesh axis runs over, the one named last changes fastest.
Arguments:
- hidden_in: bfloat16 [16384, 2048], P(('req', 'head')), may hold values from -6 to 6
- norm_gain: float32 [2048], replicated, may hold values from 0.1 to 1.9
- q_gain: float32 [128], replicated, may hold values from 0.1 to 1.9
- k_gain: float32 [128], replicated, may hold values from 0.1 to 1.9
- w_proj: bfloat16 [2048, 6144], P('req', 'head'), may hold values from -0.125 to 0.125
- cache_len: int32 [32], P('req'), may hold values from 0 to 8192, as said below
- block_table: int32 [32, 64], P('req'), may hold values from 0 to 127, as said below
- k_pool: bfloat16 [2048, 8, 128, 128], P('req', 'head'), may hold values from -410 to 410
- v_pool: bfloat16 [2048, 8, 128, 128], P('req', 'head'), may hold values from -6 to 6
Outputs:
- gated_out: bfloat16 [16384, 2048], P(('req', 'head'))
The draws below stay inside these ranges and needn't reach their ends.
Inputs may be any that keep to these rules, and one draw needn't show every extreme that they name: `cache_len`: in every draw some request has exactly 8192 cached tokens. `block_table`: the rows of requests r * 2 to r * 2 + 1 together name each of their group's 128 pages exactly once.
All inputs are finite; a program needn't handle non-finite values.
Results may differ from the reference program's by a relative error of at most 0.018.
The reference program's roundings to bfloat16 on the way (of `normed`, `queries`, `new_keys`, `new_values` and `attention`) count: a program that leaves them out, or rounds other values in their place, can miss the bound.
Values may be sent and summed in bfloat16 or wider, within the bound.
No kernel may reach another device: no remote copies, remote signals or barrier semaphores. Data moves between devices by JAX's collectives and lax.ppermute only.
A program may use at most 128 MiB of HBM per device.

```python
import math
import jax
import jax.numpy as jnp
from jax import lax

D = 2048
QH = 16
KVH = 8
HD = 128
QPK = 2
PROJ = 6144
NEW_TOK = 512
REQ_DEV = 2
MAXLEN = 8192
BLK = 128
MAXB = 64
PAGES_DEV = 128
PAGES = 2048
REQS = 32
TOKENS = 16384


def draw_cache_len(key, part):
    first_key, second_key, third_key = jax.random.split(key, 3)
    first_draw = jax.random.randint(first_key, (REQS,), 0, MAXLEN + 1)
    second_draw = jax.random.randint(second_key, (REQS,), 0, MAXLEN + 1)
    lengths = first_draw * second_draw // MAXLEN
    longest = jax.random.randint(third_key, (), 0, REQS)
    return jnp.where(jnp.arange(REQS) == longest, MAXLEN, lengths).astype(jnp.int32)


def draw_block_table(key, part):
    group_keys = jax.random.split(key, REQS // REQ_DEV)
    orders = jax.vmap(lambda group_key: jax.random.permutation(group_key, PAGES_DEV))(group_keys)
    return orders.reshape(REQS, MAXB).astype(jnp.int32)


def draw_k_pool(key, part):
    third_key = jax.random.fold_in(key, 2)
    noise = jax.random.truncated_normal(third_key, -6.0, 6.0, (PAGES, KVH, BLK, HD), jnp.float32)
    result = noise
    return result.astype(jnp.bfloat16)


def shard_levels(key, extent, cuts, least, top_value):
    def one(axis_at, parts):
        draws = jax.random.uniform(jax.random.fold_in(jax.random.fold_in(key, 6), axis_at), (parts,), jnp.float32, least / len(cuts), top_value / len(cuts))
        return jnp.repeat(jnp.exp(draws), extent[axis_at] // parts).reshape((-1,) + (1,) * (len(extent) - axis_at - 1))

    factor_of = one(*cuts[0])
    for cut in cuts[1:]:
        factor_of = factor_of * one(*cut)
    return factor_of


def bell_draw(key, dims, width, limit, cuts=(), kind=jnp.bfloat16):
    loudness = shard_levels(key, dims, cuts, -0.22, 0.18) if cuts else 1.0
    drawn = jax.random.normal(key, dims, jnp.float32) * width * loudness
    return jnp.minimum(jnp.maximum(drawn, -limit), limit).astype(kind)


def setup_inputs(seed: int = 0) -> dict:
    key_of = jax.random.split(jax.random.key(seed), 10)
    hidden_in = bell_draw(key_of[0], (TOKENS, D), 1.0, 6.0, ((0, 128),))
    norm_gain = jnp.clip(1.0 + 0.18 * jax.random.normal(key_of[1], (D,), jnp.float32), 0.1, 1.9)
    q_gain = jnp.clip(1.0 + 0.18 * jax.random.normal(key_of[2], (HD,), jnp.float32), 0.1, 1.9)
    k_gain = jnp.clip(1.0 + 0.18 * jax.random.normal(key_of[3], (HD,), jnp.float32), 0.1, 1.9)
    w_proj = bell_draw(key_of[4], (D, PROJ), D ** -0.5, 0.125, ((0, 16), (1, 8)))
    cache_len = draw_cache_len(jax.random.fold_in(key_of[9], 71), 0)
    block_table = draw_block_table(jax.random.fold_in(key_of[9], 71), 0)
    k_pool = draw_k_pool(jax.random.fold_in(key_of[9], 71), 0)
    v_pool = bell_draw(key_of[8], (PAGES, KVH, BLK, HD), 1.0, 6.0, ((0, 16), (1, 8)))
    return {"hidden_in": hidden_in, "norm_gain": norm_gain, "q_gain": q_gain, "k_gain": k_gain, "w_proj": w_proj, "cache_len": cache_len, "block_table": block_table, "k_pool": k_pool, "v_pool": v_pool}


rope_base = 1000000.0
norm_eps = 1e-06
masked_score = -1e+30

def row_norm(values, weight_gain):
    squares = lax.optimization_barrier(jnp.mean(values * values, axis=-1, keepdims=True))
    return values * lax.rsqrt(squares + norm_eps) * weight_gain

def rotate(values, positions):
    half_width = values.shape[-1] // 2
    frequency = jnp.exp(jnp.arange(half_width, dtype=jnp.float32) * (-2.0 * math.log(rope_base) / values.shape[-1]))
    angle = positions.astype(jnp.float32)[:, None] * frequency[None, :]
    bcast_shape = (angle.shape[0],) + (1,) * (values.ndim - 2) + (half_width,)
    cosine = jnp.cos(angle).reshape(bcast_shape)
    sine_wave = jnp.sin(angle).reshape(bcast_shape)
    first_half = values[..., :half_width]
    second_half = values[..., half_width:]
    return jnp.concatenate([first_half * cosine - second_half * sine_wave, second_half * cosine + first_half * sine_wave], axis=-1)

def prepare(projected, heads_here, positions, q_gain, k_gain):
    row_count = projected.shape[0]
    per_head = projected.reshape(row_count, heads_here, 2 * QPK * HD + 2 * HD)
    queries = per_head[:, :, :QPK * HD].reshape(row_count, heads_here, QPK, HD)
    key_part = per_head[:, :, QPK * HD:QPK * HD + HD]
    value_part = per_head[:, :, QPK * HD + HD:QPK * HD + 2 * HD]
    gate_part = per_head[:, :, QPK * HD + 2 * HD:].reshape(row_count, heads_here * QPK * HD)
    queries = rotate(row_norm(queries, q_gain), positions).astype(jnp.bfloat16).reshape(row_count, heads_here * QPK * HD)
    key_part = rotate(row_norm(key_part, k_gain), positions).astype(jnp.bfloat16).reshape(row_count, heads_here * HD)
    value_part = value_part.astype(jnp.bfloat16).reshape(row_count, heads_here * HD)
    return (queries, key_part, value_part, gate_part)

def update(carried, scores, values):
    running_top, running_sum, running_acc = carried
    new_top = jnp.maximum(running_top, lax.optimization_barrier(jnp.max(scores, axis=-1)))
    weights = jnp.exp(scores - new_top[..., None])
    factor = jnp.exp(running_top - new_top)
    new_sum = running_sum * factor + lax.optimization_barrier(jnp.sum(weights, axis=-1))
    rounded = lax.optimization_barrier(weights.astype(jnp.bfloat16))
    product = jnp.einsum('hrs,hsd->hrd', rounded.astype(jnp.float32), values.astype(jnp.float32), precision=lax.Precision.HIGHEST)
    return (new_top, new_sum, running_acc * factor[..., None] + product)

def attend_one(queries, key_new, value_new, length, pages, k_pool, v_pool):
    heads_here = k_pool.shape[1]
    block_len = k_pool.shape[2]
    new_count = key_new.shape[0]
    row_total = new_count * QPK
    query_rows = queries.reshape(new_count, heads_here, QPK, HD).transpose(1, 0, 2, 3).reshape(heads_here, row_total, HD).astype(jnp.float32)
    step_pages = min(pages.shape[0], max(1, 1024 // block_len))
    span_keys = step_pages * block_len
    scale_factor = 1.0 / math.sqrt(HD)

    def one_turn(turn_index, carried):
        chosen = lax.dynamic_slice_in_dim(pages, turn_index * step_pages, step_pages)
        key_block = k_pool[chosen].transpose(1, 0, 2, 3).reshape(heads_here, span_keys, HD)
        value_block = v_pool[chosen].transpose(1, 0, 2, 3).reshape(heads_here, span_keys, HD)
        scores = jnp.einsum('hrd,hsd->hrs', query_rows, key_block.astype(jnp.float32), precision=lax.Precision.HIGHEST) * scale_factor
        placed = turn_index * span_keys + jnp.arange(span_keys, dtype=jnp.int32)
        scores = jnp.where(placed[None, None, :] < length, scores, masked_score)
        return update(carried, scores, value_block)
    start_state = (jnp.full((heads_here, row_total), masked_score, jnp.float32), jnp.zeros((heads_here, row_total), jnp.float32), jnp.zeros((heads_here, row_total, HD), jnp.float32))
    turn_count = (length + span_keys - 1) // span_keys
    carried = lax.fori_loop(jnp.int32(0), turn_count, one_turn, start_state)
    new_keys = key_new.reshape(new_count, heads_here, HD).transpose(1, 0, 2)
    new_values = value_new.reshape(new_count, heads_here, HD).transpose(1, 0, 2)
    scores = jnp.einsum('hrd,hsd->hrs', query_rows, new_keys.astype(jnp.float32), precision=lax.Precision.HIGHEST) * scale_factor
    causal = jnp.arange(row_total, dtype=jnp.int32)[:, None] // QPK >= jnp.arange(new_count, dtype=jnp.int32)[None, :]
    scores = jnp.where(causal[None], scores, masked_score)
    top_row, sum_row, acc_row = update(carried, scores, new_values)
    result = acc_row / sum_row[..., None]
    return result.reshape(heads_here, new_count, QPK, HD).transpose(1, 0, 2, 3).reshape(new_count, heads_here * QPK * HD)

def reference(hidden_in, norm_gain, q_gain, k_gain, w_proj, cache_len, block_table, k_pool, v_pool):
    normed = row_norm(hidden_in.astype(jnp.float32), norm_gain).astype(jnp.bfloat16)
    projected = jnp.dot(normed, w_proj, preferred_element_type=jnp.float32)
    positions = (cache_len[:, None] + jnp.arange(NEW_TOK, dtype=jnp.int32)[None, :]).reshape(-1)
    queries, key_rows, value_rows, gate_rows = prepare(projected, KVH, positions, q_gain, k_gain)
    offsets = jnp.arange(REQS, dtype=jnp.int32) // REQ_DEV * PAGES_DEV
    pages = (block_table + offsets[:, None]).astype(jnp.int32)

    def per_request(packed):
        query_part, key_part, value_part, length, page_row = packed
        return attend_one(query_part, key_part, value_part, length, page_row, k_pool, v_pool)
    attended = lax.map(per_request, (queries.reshape(REQS, NEW_TOK, -1), key_rows.reshape(REQS, NEW_TOK, -1), value_rows.reshape(REQS, NEW_TOK, -1), cache_len, pages))
    attention = attended.reshape(TOKENS, QH * HD).astype(jnp.bfloat16)
    return (attention.astype(jnp.float32) * jax.nn.sigmoid(gate_rows)).astype(jnp.bfloat16)
```

```python
import math

import jax
import jax.numpy as jnp
from jax import lax
from jax.sharding import PartitionSpec as P

KVH = 8
HD = 128
QPK = 2
NEW_TOK = 512


rope_base = 1000000.0
norm_eps = 1e-06
masked_score = -1e30


def row_norm(values, weight_gain):
    squares = jnp.mean(values * values, axis=-1, keepdims=True)
    return values * lax.rsqrt(squares + norm_eps) * weight_gain


def rotate(values, positions):
    half_width = values.shape[-1] // 2
    frequency = jnp.exp(
        jnp.arange(half_width, dtype=jnp.float32) * (-2.0 * math.log(rope_base) / values.shape[-1])
    )
    angle = positions.astype(jnp.float32)[:, None] * frequency[None, :]
    bcast_shape = (angle.shape[0],) + (1,) * (values.ndim - 2) + (half_width,)
    cosine = jnp.cos(angle).reshape(bcast_shape)
    sine_wave = jnp.sin(angle).reshape(bcast_shape)
    first_half = values[..., :half_width]
    second_half = values[..., half_width:]
    return jnp.concatenate(
        [
            first_half * cosine - second_half * sine_wave,
            second_half * cosine + first_half * sine_wave,
        ],
        axis=-1,
    )


def prepare(projected, heads_here, positions, q_gain, k_gain):
    row_count = projected.shape[0]
    per_head = projected.reshape(row_count, heads_here, 2 * QPK * HD + 2 * HD)
    queries = per_head[:, :, : QPK * HD].reshape(row_count, heads_here, QPK, HD)
    key_part = per_head[:, :, QPK * HD : QPK * HD + HD]
    value_part = per_head[:, :, QPK * HD + HD : QPK * HD + 2 * HD]
    gate_part = per_head[:, :, QPK * HD + 2 * HD :].reshape(row_count, heads_here * QPK * HD)
    queries = (
        rotate(row_norm(queries, q_gain), positions)
        .astype(jnp.bfloat16)
        .reshape(row_count, heads_here * QPK * HD)
    )
    key_part = (
        rotate(row_norm(key_part, k_gain), positions)
        .astype(jnp.bfloat16)
        .reshape(row_count, heads_here * HD)
    )
    value_part = value_part.astype(jnp.bfloat16).reshape(row_count, heads_here * HD)
    return (queries, key_part, value_part, gate_part)


def update(carried, scores, values):
    running_top, running_sum, running_acc = carried
    new_top = jnp.maximum(running_top, jnp.max(scores, axis=-1))
    weights = jnp.exp(scores - new_top[..., None])
    factor = jnp.exp(running_top - new_top)
    new_sum = running_sum * factor + jnp.sum(weights, axis=-1)
    product = jnp.einsum(
        "hrs,hsd->hrd", weights.astype(jnp.bfloat16), values, preferred_element_type=jnp.float32
    )
    return (new_top, new_sum, running_acc * factor[..., None] + product)


def attend_one(queries, key_new, value_new, length, pages, k_pool, v_pool):
    heads_here = k_pool.shape[1]
    block_len = k_pool.shape[2]
    new_count = key_new.shape[0]
    row_total = new_count * QPK
    query_rows = (
        queries.reshape(new_count, heads_here, QPK, HD)
        .transpose(1, 0, 2, 3)
        .reshape(heads_here, row_total, HD)
    )
    step_pages = min(pages.shape[0], max(1, 1024 // block_len))
    span_keys = step_pages * block_len
    scale_factor = 1.0 / math.sqrt(HD)

    def one_turn(turn_index, carried):
        chosen = lax.dynamic_slice_in_dim(pages, turn_index * step_pages, step_pages)
        key_block = k_pool[chosen].transpose(1, 0, 2, 3).reshape(heads_here, span_keys, HD)
        value_block = v_pool[chosen].transpose(1, 0, 2, 3).reshape(heads_here, span_keys, HD)
        scores = (
            jnp.einsum("hrd,hsd->hrs", query_rows, key_block, preferred_element_type=jnp.float32)
            * scale_factor
        )
        placed = turn_index * span_keys + jnp.arange(span_keys, dtype=jnp.int32)
        scores = jnp.where(placed[None, None, :] < length, scores, masked_score)
        return update(carried, scores, value_block)

    start_state = (
        jnp.full((heads_here, row_total), masked_score, jnp.float32),
        jnp.zeros((heads_here, row_total), jnp.float32),
        jnp.zeros((heads_here, row_total, HD), jnp.float32),
    )
    turn_count = (length + span_keys - 1) // span_keys
    carried = lax.fori_loop(jnp.int32(0), turn_count, one_turn, start_state)
    new_keys = key_new.reshape(new_count, heads_here, HD).transpose(1, 0, 2)
    new_values = value_new.reshape(new_count, heads_here, HD).transpose(1, 0, 2)
    scores = (
        jnp.einsum("hrd,hsd->hrs", query_rows, new_keys, preferred_element_type=jnp.float32)
        * scale_factor
    )
    causal = (
        jnp.arange(row_total, dtype=jnp.int32)[:, None] // QPK
        >= jnp.arange(new_count, dtype=jnp.int32)[None, :]
    )
    scores = jnp.where(causal[None], scores, masked_score)
    top_row, sum_row, acc_row = update(carried, scores, new_values)
    result = acc_row / sum_row[..., None]
    return (
        result.reshape(heads_here, new_count, QPK, HD)
        .transpose(1, 0, 2, 3)
        .reshape(new_count, heads_here * QPK * HD)
    )


def attend_group(queries, key_rows, value_rows, cache_len, block_table, k_pool, v_pool):
    outputs = []
    for request in range(cache_len.shape[0]):
        row_start = request * NEW_TOK
        row_stop = row_start + NEW_TOK
        outputs.append(
            attend_one(
                queries[row_start:row_stop],
                key_rows[row_start:row_stop],
                value_rows[row_start:row_stop],
                cache_len[request],
                block_table[request],
                k_pool,
                v_pool,
            )
        )
    return jnp.concatenate(outputs, axis=0)


def lengths_of(row_ids, cache_len):
    owners = row_ids // NEW_TOK
    matches = owners[:, None] == jnp.arange(cache_len.shape[0], dtype=jnp.int32)[None, :]
    return jnp.sum(jnp.where(matches, cache_len[None, :], 0), axis=1) + row_ids % NEW_TOK


def add_rows(left_side, weight_piece):
    return jnp.dot(left_side, weight_piece, preferred_element_type=jnp.float32)


def on_device(hidden_in, norm_gain, q_gain, k_gain, w_proj, cache_len, block_table, k_pool, v_pool):
    normed = row_norm(hidden_in.astype(jnp.float32), norm_gain).astype(jnp.bfloat16)
    head_columns = lax.all_gather(w_proj, "req", axis=0, tiled=True)
    group_rows = lax.all_gather(normed, "head", axis=0, tiled=True)
    projected = add_rows(group_rows, head_columns)
    row_ids = jnp.arange(group_rows.shape[0], dtype=jnp.int32)
    positions = lengths_of(row_ids, cache_len)
    queries, key_rows, value_rows, gate_rows = prepare(projected, 1, positions, q_gain, k_gain)
    attention = attend_group(
        queries, key_rows, value_rows, cache_len, block_table, k_pool, v_pool
    ).astype(jnp.bfloat16)
    gated = (attention.astype(jnp.float32) * jax.nn.sigmoid(gate_rows)).astype(jnp.bfloat16)
    return lax.all_to_all(gated, "head", split_axis=0, concat_axis=1, tiled=True)


def solution(mesh):
    in_specs = (
        P(("req", "head"), None),
        P(),
        P(),
        P(),
        P("req", "head"),
        P("req"),
        P("req", None),
        P("req", "head", None, None),
        P("req", "head", None, None),
    )
    out_specs = P(("req", "head"), None)
    return jax.shard_map(
        on_device, mesh=mesh, in_specs=in_specs, out_specs=out_specs, check_vma=False
    )
```

```python
import math

import jax
import jax.numpy as jnp
from jax import lax
from jax.experimental import pallas as pl
from jax.experimental.pallas import tpu as pltpu
from jax.sharding import PartitionSpec as P

KVH = 8
HD = 128
QPK = 2
NEW_TOK = 512


rope_base = 1000000.0
norm_eps = 1e-06
masked_score = -1e30


def row_norm(values, weight_gain):
    squares = jnp.mean(values * values, axis=-1, keepdims=True)
    return values * lax.rsqrt(squares + norm_eps) * weight_gain


def rotate(values, positions):
    half_width = values.shape[-1] // 2
    frequency = jnp.exp(
        jnp.arange(half_width, dtype=jnp.float32) * (-2.0 * math.log(rope_base) / values.shape[-1])
    )
    angle = positions.astype(jnp.float32)[:, None] * frequency[None, :]
    bcast_shape = (angle.shape[0],) + (1,) * (values.ndim - 2) + (half_width,)
    cosine = jnp.cos(angle).reshape(bcast_shape)
    sine_wave = jnp.sin(angle).reshape(bcast_shape)
    first_half = values[..., :half_width]
    second_half = values[..., half_width:]
    return jnp.concatenate(
        [
            first_half * cosine - second_half * sine_wave,
            second_half * cosine + first_half * sine_wave,
        ],
        axis=-1,
    )


def prepare(projected, heads_here, positions, q_gain, k_gain):
    row_count = projected.shape[0]
    per_head = projected.reshape(row_count, heads_here, 2 * QPK * HD + 2 * HD)
    queries = per_head[:, :, : QPK * HD].reshape(row_count, heads_here, QPK, HD)
    key_part = per_head[:, :, QPK * HD : QPK * HD + HD]
    value_part = per_head[:, :, QPK * HD + HD : QPK * HD + 2 * HD]
    gate_part = per_head[:, :, QPK * HD + 2 * HD :].reshape(row_count, heads_here * QPK * HD)
    queries = (
        rotate(row_norm(queries, q_gain), positions)
        .astype(jnp.bfloat16)
        .reshape(row_count, heads_here * QPK * HD)
    )
    key_part = (
        rotate(row_norm(key_part, k_gain), positions)
        .astype(jnp.bfloat16)
        .reshape(row_count, heads_here * HD)
    )
    value_part = value_part.astype(jnp.bfloat16).reshape(row_count, heads_here * HD)
    return (queries, key_part, value_part, gate_part)


def update(carried, scores, values):
    running_top, running_sum, running_acc = carried
    new_top = jnp.maximum(running_top, jnp.max(scores, axis=-1))
    weights = jnp.exp(scores - new_top[..., None])
    factor = jnp.exp(running_top - new_top)
    new_sum = running_sum * factor + jnp.sum(weights, axis=-1)
    product = jnp.einsum(
        "hrs,hsd->hrd", weights.astype(jnp.bfloat16), values, preferred_element_type=jnp.float32
    )
    return (new_top, new_sum, running_acc * factor[..., None] + product)


def attend_one(queries, key_new, value_new, length, pages, k_pool, v_pool):
    heads_here = k_pool.shape[1]
    block_len = k_pool.shape[2]
    new_count = key_new.shape[0]
    row_total = new_count * QPK
    query_rows = (
        queries.reshape(new_count, heads_here, QPK, HD)
        .transpose(1, 0, 2, 3)
        .reshape(heads_here, row_total, HD)
    )
    step_pages = min(pages.shape[0], max(1, 1024 // block_len))
    span_keys = step_pages * block_len
    scale_factor = 1.0 / math.sqrt(HD)

    def one_turn(turn_index, carried):
        chosen = lax.dynamic_slice_in_dim(pages, turn_index * step_pages, step_pages)
        key_block = k_pool[chosen].transpose(1, 0, 2, 3).reshape(heads_here, span_keys, HD)
        value_block = v_pool[chosen].transpose(1, 0, 2, 3).reshape(heads_here, span_keys, HD)
        scores = (
            jnp.einsum("hrd,hsd->hrs", query_rows, key_block, preferred_element_type=jnp.float32)
            * scale_factor
        )
        placed = turn_index * span_keys + jnp.arange(span_keys, dtype=jnp.int32)
        scores = jnp.where(placed[None, None, :] < length, scores, masked_score)
        return update(carried, scores, value_block)

    start_state = (
        jnp.full((heads_here, row_total), masked_score, jnp.float32),
        jnp.zeros((heads_here, row_total), jnp.float32),
        jnp.zeros((heads_here, row_total, HD), jnp.float32),
    )
    turn_count = (length + span_keys - 1) // span_keys
    carried = lax.fori_loop(jnp.int32(0), turn_count, one_turn, start_state)
    new_keys = key_new.reshape(new_count, heads_here, HD).transpose(1, 0, 2)
    new_values = value_new.reshape(new_count, heads_here, HD).transpose(1, 0, 2)
    scores = (
        jnp.einsum("hrd,hsd->hrs", query_rows, new_keys, preferred_element_type=jnp.float32)
        * scale_factor
    )
    causal = (
        jnp.arange(row_total, dtype=jnp.int32)[:, None] // QPK
        >= jnp.arange(new_count, dtype=jnp.int32)[None, :]
    )
    scores = jnp.where(causal[None], scores, masked_score)
    top_row, sum_row, acc_row = update(carried, scores, new_values)
    result = acc_row / sum_row[..., None]
    return (
        result.reshape(heads_here, new_count, QPK, HD)
        .transpose(1, 0, 2, 3)
        .reshape(new_count, heads_here * QPK * HD)
    )


def attend_group(queries, key_rows, value_rows, cache_len, block_table, k_pool, v_pool):
    outputs = []
    for request in range(cache_len.shape[0]):
        row_start = request * NEW_TOK
        row_stop = row_start + NEW_TOK
        outputs.append(
            attend_one(
                queries[row_start:row_stop],
                key_rows[row_start:row_stop],
                value_rows[row_start:row_stop],
                cache_len[request],
                block_table[request],
                k_pool,
                v_pool,
            )
        )
    return jnp.concatenate(outputs, axis=0)


PAGES_STEP = 8


def flash_kernel(lens_ref, table_ref, q_ref, kn_ref, vn_ref, *rest):
    key_pages = rest[:PAGES_STEP]
    value_pages = rest[PAGES_STEP : 2 * PAGES_STEP]
    out_ref, top_sc, sum_sc, acc_sc = rest[2 * PAGES_STEP :]
    request = pl.program_id(0)
    turn = pl.program_id(1)
    last_turn = pl.num_programs(1) - 1
    length = lens_ref[request]
    rows = q_ref.shape[0]
    span = PAGES_STEP * key_pages[0].shape[0]
    scale_factor = 1.0 / math.sqrt(HD)

    @pl.when(turn == 0)
    def _():
        top_sc[...] = jnp.full(top_sc.shape, masked_score, jnp.float32)
        sum_sc[...] = jnp.zeros(sum_sc.shape, jnp.float32)
        acc_sc[...] = jnp.zeros(acc_sc.shape, jnp.float32)

    def absorb(keys, values, keep):
        for a in range(QPK):
            query = q_ref[:, a * HD : (a + 1) * HD]
            scores = (
                lax.dot_general(
                    query, keys, (((1,), (1,)), ((), ())), preferred_element_type=jnp.float32
                )
                * scale_factor
            )
            scores = jnp.where(keep, scores, masked_score)
            running_top = top_sc[a]
            new_top = jnp.maximum(running_top, jnp.max(scores, axis=1, keepdims=True))
            weights = jnp.exp(scores - new_top)
            factor = jnp.exp(running_top - new_top)
            sum_sc[a] = sum_sc[a] * factor + jnp.sum(weights, axis=1, keepdims=True)
            product = jnp.dot(
                weights.astype(jnp.bfloat16), values, preferred_element_type=jnp.float32
            )
            acc_sc[a] = acc_sc[a] * factor + product
            top_sc[a] = new_top

    @pl.when(jnp.logical_and(turn < last_turn, turn * span < length))
    def _():
        keys = jnp.concatenate([page[...] for page in key_pages], axis=0)
        values = jnp.concatenate([page[...] for page in value_pages], axis=0)
        placed = turn * span + lax.broadcasted_iota(jnp.int32, (1, span), 1)
        absorb(keys, values, placed < length)

    @pl.when(turn == last_turn)
    def _():
        causal = lax.broadcasted_iota(jnp.int32, (rows, rows), 0) >= lax.broadcasted_iota(
            jnp.int32, (rows, rows), 1
        )
        absorb(kn_ref[...], vn_ref[...], causal)
        for a in range(QPK):
            out_ref[:, a * HD : (a + 1) * HD] = (acc_sc[a] / sum_sc[a]).astype(out_ref.dtype)


def flash_attend(queries, key_rows, value_rows, cache_len, block_table, k_pool, v_pool):
    requests, table_width = block_table.shape
    pages_here, _, block_len, _ = k_pool.shape
    key_pages = k_pool.reshape(pages_here, block_len, HD)
    value_pages = v_pool.reshape(pages_here, block_len, HD)
    turns = table_width // PAGES_STEP + 1
    rows = queries.shape[0] // requests

    def page_spec(slot):
        def index_map(request, turn, lens_ref, table_ref):
            blocks = (lens_ref[request] + block_len - 1) // block_len
            chosen = jnp.minimum(turn * PAGES_STEP + slot, jnp.maximum(blocks - 1, 0))
            return (table_ref[request * table_width + chosen], 0, 0)

        return pl.BlockSpec((None, block_len, HD), index_map)

    def row_spec(width):
        return pl.BlockSpec((rows, width), lambda request, turn, lens_ref, table_ref: (request, 0))

    grid_spec = pltpu.PrefetchScalarGridSpec(
        num_scalar_prefetch=2,
        grid=(requests, turns),
        in_specs=[row_spec(QPK * HD), row_spec(HD), row_spec(HD)]
        + [page_spec(slot) for slot in range(PAGES_STEP)] * 2,
        out_specs=row_spec(QPK * HD),
        scratch_shapes=[
            pltpu.VMEM((QPK, rows, 1), jnp.float32),
            pltpu.VMEM((QPK, rows, 1), jnp.float32),
            pltpu.VMEM((QPK, rows, HD), jnp.float32),
        ],
    )
    return pl.pallas_call(
        flash_kernel,
        grid_spec=grid_spec,
        out_shape=jax.ShapeDtypeStruct((queries.shape[0], QPK * HD), jnp.bfloat16),
        compiler_params=pltpu.CompilerParams(dimension_semantics=("arbitrary", "arbitrary")),
    )(
        cache_len,
        block_table.reshape(-1),
        queries,
        key_rows,
        value_rows,
        *([key_pages] * PAGES_STEP),
        *([value_pages] * PAGES_STEP),
    )


def lengths_of(row_ids, cache_len):
    owners = row_ids // NEW_TOK
    matches = owners[:, None] == jnp.arange(cache_len.shape[0], dtype=jnp.int32)[None, :]
    return jnp.sum(jnp.where(matches, cache_len[None, :], 0), axis=1) + row_ids % NEW_TOK


def add_rows(left_side, weight_piece):
    return jnp.dot(left_side, weight_piece, preferred_element_type=jnp.float32)


def on_device(hidden_in, norm_gain, q_gain, k_gain, w_proj, cache_len, block_table, k_pool, v_pool):
    normed = row_norm(hidden_in.astype(jnp.float32), norm_gain).astype(jnp.bfloat16)
    head_columns = lax.all_gather(w_proj, "req", axis=0, tiled=True)
    group_rows = lax.all_gather(normed, "head", axis=0, tiled=True)
    projected = add_rows(group_rows, head_columns)
    row_ids = jnp.arange(group_rows.shape[0], dtype=jnp.int32)
    positions = lengths_of(row_ids, cache_len)
    queries, key_rows, value_rows, gate_rows = prepare(projected, 1, positions, q_gain, k_gain)
    attention = flash_attend(
        queries, key_rows, value_rows, cache_len, block_table, k_pool, v_pool
    )
    gated = (attention.astype(jnp.float32) * jax.nn.sigmoid(gate_rows)).astype(jnp.bfloat16)
    return lax.all_to_all(gated, "head", split_axis=0, concat_axis=1, tiled=True)


def solution(mesh):
    in_specs = (
        P(("req", "head"), None),
        P(),
        P(),
        P(),
        P("req", "head"),
        P("req"),
        P("req", None),
        P("req", "head", None, None),
        P("req", "head", None, None),
    )
    out_specs = P(("req", "head"), None)
    return jax.shard_map(
        on_device, mesh=mesh, in_specs=in_specs, out_specs=out_specs, check_vma=False
    )
```

```python
import math

import jax
import jax.numpy as jnp
from jax import lax
from jax.experimental import pallas as pl
from jax.experimental.pallas import tpu as pltpu
from jax.sharding import PartitionSpec as P

KVH = 8
HD = 128
QPK = 2
NEW_TOK = 512


rope_base = 1000000.0
norm_eps = 1e-06
masked_score = -1e30


def row_norm(values, weight_gain):
    squares = jnp.mean(values * values, axis=-1, keepdims=True)
    return values * lax.rsqrt(squares + norm_eps) * weight_gain


def rotate(values, positions):
    half_width = values.shape[-1] // 2
    frequency = jnp.exp(
        jnp.arange(half_width, dtype=jnp.float32) * (-2.0 * math.log(rope_base) / values.shape[-1])
    )
    angle = positions.astype(jnp.float32)[:, None] * frequency[None, :]
    bcast_shape = (angle.shape[0],) + (1,) * (values.ndim - 2) + (half_width,)
    cosine = jnp.cos(angle).reshape(bcast_shape)
    sine_wave = jnp.sin(angle).reshape(bcast_shape)
    first_half = values[..., :half_width]
    second_half = values[..., half_width:]
    return jnp.concatenate(
        [
            first_half * cosine - second_half * sine_wave,
            second_half * cosine + first_half * sine_wave,
        ],
        axis=-1,
    )


def prepare(projected, heads_here, positions, q_gain, k_gain):
    row_count = projected.shape[0]
    per_head = projected.reshape(row_count, heads_here, 2 * QPK * HD + 2 * HD)
    queries = per_head[:, :, : QPK * HD].reshape(row_count, heads_here, QPK, HD)
    key_part = per_head[:, :, QPK * HD : QPK * HD + HD]
    value_part = per_head[:, :, QPK * HD + HD : QPK * HD + 2 * HD]
    gate_part = per_head[:, :, QPK * HD + 2 * HD :].reshape(row_count, heads_here * QPK * HD)
    queries = (
        rotate(row_norm(queries, q_gain), positions)
        .astype(jnp.bfloat16)
        .reshape(row_count, heads_here * QPK * HD)
    )
    key_part = (
        rotate(row_norm(key_part, k_gain), positions)
        .astype(jnp.bfloat16)
        .reshape(row_count, heads_here * HD)
    )
    value_part = value_part.astype(jnp.bfloat16).reshape(row_count, heads_here * HD)
    return (queries, key_part, value_part, gate_part)


def update(carried, scores, values):
    running_top, running_sum, running_acc = carried
    new_top = jnp.maximum(running_top, jnp.max(scores, axis=-1))
    weights = jnp.exp(scores - new_top[..., None])
    factor = jnp.exp(running_top - new_top)
    new_sum = running_sum * factor + jnp.sum(weights, axis=-1)
    product = jnp.einsum(
        "hrs,hsd->hrd", weights.astype(jnp.bfloat16), values, preferred_element_type=jnp.float32
    )
    return (new_top, new_sum, running_acc * factor[..., None] + product)


def attend_one(queries, key_new, value_new, length, pages, k_pool, v_pool):
    heads_here = k_pool.shape[1]
    block_len = k_pool.shape[2]
    new_count = key_new.shape[0]
    row_total = new_count * QPK
    query_rows = (
        queries.reshape(new_count, heads_here, QPK, HD)
        .transpose(1, 0, 2, 3)
        .reshape(heads_here, row_total, HD)
    )
    step_pages = min(pages.shape[0], max(1, 1024 // block_len))
    span_keys = step_pages * block_len
    scale_factor = 1.0 / math.sqrt(HD)

    def one_turn(turn_index, carried):
        chosen = lax.dynamic_slice_in_dim(pages, turn_index * step_pages, step_pages)
        key_block = k_pool[chosen].transpose(1, 0, 2, 3).reshape(heads_here, span_keys, HD)
        value_block = v_pool[chosen].transpose(1, 0, 2, 3).reshape(heads_here, span_keys, HD)
        scores = (
            jnp.einsum("hrd,hsd->hrs", query_rows, key_block, preferred_element_type=jnp.float32)
            * scale_factor
        )
        placed = turn_index * span_keys + jnp.arange(span_keys, dtype=jnp.int32)
        scores = jnp.where(placed[None, None, :] < length, scores, masked_score)
        return update(carried, scores, value_block)

    start_state = (
        jnp.full((heads_here, row_total), masked_score, jnp.float32),
        jnp.zeros((heads_here, row_total), jnp.float32),
        jnp.zeros((heads_here, row_total, HD), jnp.float32),
    )
    turn_count = (length + span_keys - 1) // span_keys
    carried = lax.fori_loop(jnp.int32(0), turn_count, one_turn, start_state)
    new_keys = key_new.reshape(new_count, heads_here, HD).transpose(1, 0, 2)
    new_values = value_new.reshape(new_count, heads_here, HD).transpose(1, 0, 2)
    scores = (
        jnp.einsum("hrd,hsd->hrs", query_rows, new_keys, preferred_element_type=jnp.float32)
        * scale_factor
    )
    causal = (
        jnp.arange(row_total, dtype=jnp.int32)[:, None] // QPK
        >= jnp.arange(new_count, dtype=jnp.int32)[None, :]
    )
    scores = jnp.where(causal[None], scores, masked_score)
    top_row, sum_row, acc_row = update(carried, scores, new_values)
    result = acc_row / sum_row[..., None]
    return (
        result.reshape(heads_here, new_count, QPK, HD)
        .transpose(1, 0, 2, 3)
        .reshape(new_count, heads_here * QPK * HD)
    )


def attend_group(queries, key_rows, value_rows, cache_len, block_table, k_pool, v_pool):
    outputs = []
    for request in range(cache_len.shape[0]):
        row_start = request * NEW_TOK
        row_stop = row_start + NEW_TOK
        outputs.append(
            attend_one(
                queries[row_start:row_stop],
                key_rows[row_start:row_stop],
                value_rows[row_start:row_stop],
                cache_len[request],
                block_table[request],
                k_pool,
                v_pool,
            )
        )
    return jnp.concatenate(outputs, axis=0)


PAGES_STEP = 8


def flash_kernel(lens_ref, table_ref, q_ref, kn_ref, vn_ref, *rest):
    key_pages = rest[:PAGES_STEP]
    value_pages = rest[PAGES_STEP : 2 * PAGES_STEP]
    out_ref, top_sc, sum_sc, acc_sc = rest[2 * PAGES_STEP :]
    request = pl.program_id(0)
    turn = pl.program_id(1)
    last_turn = pl.num_programs(1) - 1
    length = lens_ref[request]
    rows = q_ref.shape[0]
    span = PAGES_STEP * key_pages[0].shape[0]
    scale_factor = 1.0 / math.sqrt(HD)

    @pl.when(turn == 0)
    def _():
        top_sc[...] = jnp.full(top_sc.shape, masked_score, jnp.float32)
        sum_sc[...] = jnp.zeros(sum_sc.shape, jnp.float32)
        acc_sc[...] = jnp.zeros(acc_sc.shape, jnp.float32)

    def absorb(keys, values, keep):
        for a in range(QPK):
            query = q_ref[:, a * HD : (a + 1) * HD]
            scores = (
                lax.dot_general(
                    query, keys, (((1,), (1,)), ((), ())), preferred_element_type=jnp.float32
                )
                * scale_factor
            )
            scores = jnp.where(keep, scores, masked_score)
            running_top = top_sc[a]
            new_top = jnp.maximum(running_top, jnp.max(scores, axis=1, keepdims=True))
            weights = jnp.exp(scores - new_top)
            factor = jnp.exp(running_top - new_top)
            sum_sc[a] = sum_sc[a] * factor + jnp.sum(weights, axis=1, keepdims=True)
            product = jnp.dot(
                weights.astype(jnp.bfloat16), values, preferred_element_type=jnp.float32
            )
            acc_sc[a] = acc_sc[a] * factor + product
            top_sc[a] = new_top

    @pl.when(jnp.logical_and(turn < last_turn, turn * span < length))
    def _():
        keys = jnp.concatenate([page[...] for page in key_pages], axis=0)
        values = jnp.concatenate([page[...] for page in value_pages], axis=0)
        placed = turn * span + lax.broadcasted_iota(jnp.int32, (1, span), 1)
        absorb(keys, values, placed < length)

    @pl.when(turn == last_turn)
    def _():
        causal = lax.broadcasted_iota(jnp.int32, (rows, rows), 0) >= lax.broadcasted_iota(
            jnp.int32, (rows, rows), 1
        )
        absorb(kn_ref[...], vn_ref[...], causal)
        for a in range(QPK):
            out_ref[:, a * HD : (a + 1) * HD] = (acc_sc[a] / sum_sc[a]).astype(out_ref.dtype)


def flash_attend(queries, key_rows, value_rows, cache_len, block_table, k_pool, v_pool):
    requests, table_width = block_table.shape
    pages_here, _, block_len, _ = k_pool.shape
    key_pages = k_pool.reshape(pages_here, block_len, HD)
    value_pages = v_pool.reshape(pages_here, block_len, HD)
    turns = table_width // PAGES_STEP + 1
    rows = queries.shape[0] // requests

    def page_spec(slot):
        def index_map(request, turn, lens_ref, table_ref):
            blocks = (lens_ref[request] + block_len - 1) // block_len
            chosen = jnp.minimum(turn * PAGES_STEP + slot, jnp.maximum(blocks - 1, 0))
            return (table_ref[request * table_width + chosen], 0, 0)

        return pl.BlockSpec((None, block_len, HD), index_map)

    def row_spec(width):
        return pl.BlockSpec((rows, width), lambda request, turn, lens_ref, table_ref: (request, 0))

    grid_spec = pltpu.PrefetchScalarGridSpec(
        num_scalar_prefetch=2,
        grid=(requests, turns),
        in_specs=[row_spec(QPK * HD), row_spec(HD), row_spec(HD)]
        + [page_spec(slot) for slot in range(PAGES_STEP)] * 2,
        out_specs=row_spec(QPK * HD),
        scratch_shapes=[
            pltpu.VMEM((QPK, rows, 1), jnp.float32),
            pltpu.VMEM((QPK, rows, 1), jnp.float32),
            pltpu.VMEM((QPK, rows, HD), jnp.float32),
        ],
    )
    return pl.pallas_call(
        flash_kernel,
        grid_spec=grid_spec,
        out_shape=jax.ShapeDtypeStruct((queries.shape[0], QPK * HD), jnp.bfloat16),
        compiler_params=pltpu.CompilerParams(dimension_semantics=("arbitrary", "arbitrary")),
    )(
        cache_len,
        block_table.reshape(-1),
        queries,
        key_rows,
        value_rows,
        *([key_pages] * PAGES_STEP),
        *([value_pages] * PAGES_STEP),
    )


def lengths_of(row_ids, cache_len):
    owners = row_ids // NEW_TOK
    matches = owners[:, None] == jnp.arange(cache_len.shape[0], dtype=jnp.int32)[None, :]
    return jnp.sum(jnp.where(matches, cache_len[None, :], 0), axis=1) + row_ids % NEW_TOK


def add_rows(left_side, weight_piece):
    return jnp.dot(left_side, weight_piece, preferred_element_type=jnp.float32)


def on_device(hidden_in, norm_gain, q_gain, k_gain, w_proj, cache_len, block_table, k_pool, v_pool):
    normed = row_norm(hidden_in.astype(jnp.float32), norm_gain).astype(jnp.bfloat16)
    req_count = lax.axis_size("req")
    copies = jnp.broadcast_to(w_proj[None], (req_count,) + w_proj.shape)
    head_columns = lax.all_to_all(copies, "req", 0, 0, tiled=True).reshape(-1, w_proj.shape[1])
    group_rows = lax.all_gather(normed, "head", axis=0, tiled=True)
    projected = add_rows(group_rows, head_columns)
    row_ids = jnp.arange(group_rows.shape[0], dtype=jnp.int32)
    positions = lengths_of(row_ids, cache_len)
    queries, key_rows, value_rows, gate_rows = prepare(projected, 1, positions, q_gain, k_gain)
    attention = flash_attend(
        queries, key_rows, value_rows, cache_len, block_table, k_pool, v_pool
    )
    gated = (attention.astype(jnp.float32) * jax.nn.sigmoid(gate_rows)).astype(jnp.bfloat16)
    return lax.all_to_all(gated, "head", split_axis=0, concat_axis=1, tiled=True)


def solution(mesh):
    in_specs = (
        P(("req", "head"), None),
        P(),
        P(),
        P(),
        P("req", "head"),
        P("req"),
        P("req", None),
        P("req", "head", None, None),
        P("req", "head", None, None),
    )
    out_specs = P(("req", "head"), None)
    return jax.shard_map(
        on_device, mesh=mesh, in_specs=in_specs, out_specs=out_specs, check_vma=False
    )
```

```python
import math

import jax
import jax.numpy as jnp
from jax import lax
from jax.experimental import pallas as pl
from jax.experimental.pallas import tpu as pltpu
from jax.sharding import PartitionSpec as P

KVH = 8
HD = 128
QPK = 2
NEW_TOK = 512


rope_base = 1000000.0
norm_eps = 1e-06
masked_score = -1e30


def row_norm(values, weight_gain):
    squares = jnp.mean(values * values, axis=-1, keepdims=True)
    return values * lax.rsqrt(squares + norm_eps) * weight_gain


def rotate(values, positions):
    half_width = values.shape[-1] // 2
    frequency = jnp.exp(
        jnp.arange(half_width, dtype=jnp.float32) * (-2.0 * math.log(rope_base) / values.shape[-1])
    )
    angle = positions.astype(jnp.float32)[:, None] * frequency[None, :]
    bcast_shape = (angle.shape[0],) + (1,) * (values.ndim - 2) + (half_width,)
    cosine = jnp.cos(angle).reshape(bcast_shape)
    sine_wave = jnp.sin(angle).reshape(bcast_shape)
    first_half = values[..., :half_width]
    second_half = values[..., half_width:]
    return jnp.concatenate(
        [
            first_half * cosine - second_half * sine_wave,
            second_half * cosine + first_half * sine_wave,
        ],
        axis=-1,
    )


def prepare(projected, positions, q_gain, k_gain):
    row_count = projected.shape[0]
    queries = projected[:, : QPK * HD].reshape(row_count, QPK, HD)
    key_part = projected[:, QPK * HD : QPK * HD + HD]
    value_part = projected[:, QPK * HD + HD : QPK * HD + 2 * HD]
    queries = (
        rotate(row_norm(queries, q_gain), positions)
        .astype(jnp.bfloat16)
        .reshape(row_count, QPK * HD)
    )
    key_part = rotate(row_norm(key_part, k_gain), positions).astype(jnp.bfloat16)
    value_part = value_part.astype(jnp.bfloat16)
    return (queries, key_part, value_part)


def update(carried, scores, values):
    running_top, running_sum, running_acc = carried
    new_top = jnp.maximum(running_top, jnp.max(scores, axis=-1))
    weights = jnp.exp(scores - new_top[..., None])
    factor = jnp.exp(running_top - new_top)
    new_sum = running_sum * factor + jnp.sum(weights, axis=-1)
    product = jnp.einsum(
        "hrs,hsd->hrd", weights.astype(jnp.bfloat16), values, preferred_element_type=jnp.float32
    )
    return (new_top, new_sum, running_acc * factor[..., None] + product)


def attend_one(queries, key_new, value_new, length, pages, k_pool, v_pool):
    heads_here = k_pool.shape[1]
    block_len = k_pool.shape[2]
    new_count = key_new.shape[0]
    row_total = new_count * QPK
    query_rows = (
        queries.reshape(new_count, heads_here, QPK, HD)
        .transpose(1, 0, 2, 3)
        .reshape(heads_here, row_total, HD)
    )
    step_pages = min(pages.shape[0], max(1, 1024 // block_len))
    span_keys = step_pages * block_len
    scale_factor = 1.0 / math.sqrt(HD)

    def one_turn(turn_index, carried):
        chosen = lax.dynamic_slice_in_dim(pages, turn_index * step_pages, step_pages)
        key_block = k_pool[chosen].transpose(1, 0, 2, 3).reshape(heads_here, span_keys, HD)
        value_block = v_pool[chosen].transpose(1, 0, 2, 3).reshape(heads_here, span_keys, HD)
        scores = (
            jnp.einsum("hrd,hsd->hrs", query_rows, key_block, preferred_element_type=jnp.float32)
            * scale_factor
        )
        placed = turn_index * span_keys + jnp.arange(span_keys, dtype=jnp.int32)
        scores = jnp.where(placed[None, None, :] < length, scores, masked_score)
        return update(carried, scores, value_block)

    start_state = (
        jnp.full((heads_here, row_total), masked_score, jnp.float32),
        jnp.zeros((heads_here, row_total), jnp.float32),
        jnp.zeros((heads_here, row_total, HD), jnp.float32),
    )
    turn_count = (length + span_keys - 1) // span_keys
    carried = lax.fori_loop(jnp.int32(0), turn_count, one_turn, start_state)
    new_keys = key_new.reshape(new_count, heads_here, HD).transpose(1, 0, 2)
    new_values = value_new.reshape(new_count, heads_here, HD).transpose(1, 0, 2)
    scores = (
        jnp.einsum("hrd,hsd->hrs", query_rows, new_keys, preferred_element_type=jnp.float32)
        * scale_factor
    )
    causal = (
        jnp.arange(row_total, dtype=jnp.int32)[:, None] // QPK
        >= jnp.arange(new_count, dtype=jnp.int32)[None, :]
    )
    scores = jnp.where(causal[None], scores, masked_score)
    top_row, sum_row, acc_row = update(carried, scores, new_values)
    result = acc_row / sum_row[..., None]
    return (
        result.reshape(heads_here, new_count, QPK, HD)
        .transpose(1, 0, 2, 3)
        .reshape(new_count, heads_here * QPK * HD)
    )


def attend_group(queries, key_rows, value_rows, cache_len, block_table, k_pool, v_pool):
    outputs = []
    for request in range(cache_len.shape[0]):
        row_start = request * NEW_TOK
        row_stop = row_start + NEW_TOK
        outputs.append(
            attend_one(
                queries[row_start:row_stop],
                key_rows[row_start:row_stop],
                value_rows[row_start:row_stop],
                cache_len[request],
                block_table[request],
                k_pool,
                v_pool,
            )
        )
    return jnp.concatenate(outputs, axis=0)


PAGES_STEP = 8


def flash_kernel(lens_ref, table_ref, q_ref, kn_ref, vn_ref, *rest):
    key_pages = rest[:PAGES_STEP]
    value_pages = rest[PAGES_STEP : 2 * PAGES_STEP]
    out_ref, top_sc, sum_sc, acc_sc = rest[2 * PAGES_STEP :]
    request = pl.program_id(0)
    turn = pl.program_id(1)
    last_turn = pl.num_programs(1) - 1
    length = lens_ref[request]
    rows = q_ref.shape[0]
    span = PAGES_STEP * key_pages[0].shape[0]
    scale_factor = 1.0 / math.sqrt(HD)

    @pl.when(turn == 0)
    def _():
        top_sc[...] = jnp.full(top_sc.shape, masked_score, jnp.float32)
        sum_sc[...] = jnp.zeros(sum_sc.shape, jnp.float32)
        acc_sc[...] = jnp.zeros(acc_sc.shape, jnp.float32)

    def absorb(keys, values, keep):
        for a in range(QPK):
            query = q_ref[:, a * HD : (a + 1) * HD]
            scores = (
                lax.dot_general(
                    query, keys, (((1,), (1,)), ((), ())), preferred_element_type=jnp.float32
                )
                * scale_factor
            )
            if keep is not None:
                scores = jnp.where(keep, scores, masked_score)
            running_top = top_sc[a]
            new_top = jnp.maximum(running_top, jnp.max(scores, axis=1, keepdims=True))
            weights = jnp.exp(scores - new_top)
            factor = jnp.exp(running_top - new_top)
            sum_sc[a] = sum_sc[a] * factor + jnp.sum(weights, axis=1, keepdims=True)
            product = jnp.dot(
                weights.astype(jnp.bfloat16), values, preferred_element_type=jnp.float32
            )
            acc_sc[a] = acc_sc[a] * factor + product
            top_sc[a] = new_top

    def cached(masked):
        keys = jnp.concatenate([page[...] for page in key_pages], axis=0)
        values = jnp.concatenate([page[...] for page in value_pages], axis=0)
        if masked:
            placed = turn * span + lax.broadcasted_iota(jnp.int32, (1, span), 1)
            absorb(keys, values, placed < length)
        else:
            absorb(keys, values, None)

    cached_turn = turn < last_turn
    whole = (turn + 1) * span <= length
    partial = jnp.logical_and(turn * span < length, jnp.logical_not(whole))
    pl.when(jnp.logical_and(cached_turn, whole))(lambda: cached(False))
    pl.when(jnp.logical_and(cached_turn, partial))(lambda: cached(True))

    @pl.when(turn == last_turn)
    def _():
        causal = lax.broadcasted_iota(jnp.int32, (rows, rows), 0) >= lax.broadcasted_iota(
            jnp.int32, (rows, rows), 1
        )
        absorb(kn_ref[...], vn_ref[...], causal)
        for a in range(QPK):
            out_ref[:, a * HD : (a + 1) * HD] = (acc_sc[a] / sum_sc[a]).astype(out_ref.dtype)


def flash_attend(queries, key_rows, value_rows, cache_len, block_table, k_pool, v_pool):
    requests, table_width = block_table.shape
    pages_here, _, block_len, _ = k_pool.shape
    key_pages = k_pool.reshape(pages_here, block_len, HD)
    value_pages = v_pool.reshape(pages_here, block_len, HD)
    turns = table_width // PAGES_STEP + 1
    rows = queries.shape[0] // requests

    def page_spec(slot):
        def index_map(request, turn, lens_ref, table_ref):
            blocks = (lens_ref[request] + block_len - 1) // block_len
            chosen = jnp.minimum(turn * PAGES_STEP + slot, jnp.maximum(blocks - 1, 0))
            return (table_ref[request * table_width + chosen], 0, 0)

        return pl.BlockSpec((None, block_len, HD), index_map)

    def row_spec(width):
        return pl.BlockSpec((rows, width), lambda request, turn, lens_ref, table_ref: (request, 0))

    grid_spec = pltpu.PrefetchScalarGridSpec(
        num_scalar_prefetch=2,
        grid=(requests, turns),
        in_specs=[row_spec(QPK * HD), row_spec(HD), row_spec(HD)]
        + [page_spec(slot) for slot in range(PAGES_STEP)] * 2,
        out_specs=row_spec(QPK * HD),
        scratch_shapes=[
            pltpu.VMEM((QPK, rows, 1), jnp.float32),
            pltpu.VMEM((QPK, rows, 1), jnp.float32),
            pltpu.VMEM((QPK, rows, HD), jnp.float32),
        ],
    )
    return pl.pallas_call(
        flash_kernel,
        grid_spec=grid_spec,
        out_shape=jax.ShapeDtypeStruct((queries.shape[0], QPK * HD), jnp.bfloat16),
        compiler_params=pltpu.CompilerParams(dimension_semantics=("arbitrary", "arbitrary")),
    )(
        cache_len,
        block_table.reshape(-1),
        queries,
        key_rows,
        value_rows,
        *([key_pages] * PAGES_STEP),
        *([value_pages] * PAGES_STEP),
    )


def lengths_of(row_ids, cache_len):
    owners = row_ids // NEW_TOK
    matches = owners[:, None] == jnp.arange(cache_len.shape[0], dtype=jnp.int32)[None, :]
    return jnp.sum(jnp.where(matches, cache_len[None, :], 0), axis=1) + row_ids % NEW_TOK


def add_rows(left_side, weight_piece):
    return jnp.dot(left_side, weight_piece, preferred_element_type=jnp.float32)


def gather_columns(piece):
    req_count = lax.axis_size("req")
    copies = jnp.broadcast_to(piece[None], (req_count,) + piece.shape)
    return lax.all_to_all(copies, "req", 0, 0, tiled=True).reshape(-1, piece.shape[1])


def on_device(hidden_in, norm_gain, q_gain, k_gain, w_proj, cache_len, block_table, k_pool, v_pool):
    normed = row_norm(hidden_in.astype(jnp.float32), norm_gain).astype(jnp.bfloat16)
    split = QPK * HD + 2 * HD
    attend_columns = gather_columns(w_proj[:, :split])
    gate_columns = gather_columns(w_proj[:, split:])
    group_rows = lax.all_gather(normed, "head", axis=0, tiled=True)
    projected = add_rows(group_rows, attend_columns)
    row_ids = jnp.arange(group_rows.shape[0], dtype=jnp.int32)
    positions = lengths_of(row_ids, cache_len)
    queries, key_rows, value_rows = prepare(projected, positions, q_gain, k_gain)
    attention = flash_attend(
        queries, key_rows, value_rows, cache_len, block_table, k_pool, v_pool
    )
    gate_rows = add_rows(group_rows, gate_columns)
    gated = (attention.astype(jnp.float32) * jax.nn.sigmoid(gate_rows)).astype(jnp.bfloat16)
    return lax.all_to_all(gated, "head", split_axis=0, concat_axis=1, tiled=True)


def solution(mesh):
    in_specs = (
        P(("req", "head"), None),
        P(),
        P(),
        P(),
        P("req", "head"),
        P("req"),
        P("req", None),
        P("req", "head", None, None),
        P("req", "head", None, None),
    )
    out_specs = P(("req", "head"), None)
    return jax.shard_map(
        on_device, mesh=mesh, in_specs=in_specs, out_specs=out_specs, check_vma=False
    )
```

```python
import math

import jax
import jax.numpy as jnp
from jax import lax
from jax.experimental import pallas as pl
from jax.experimental.pallas import tpu as pltpu
from jax.sharding import PartitionSpec as P

KVH = 8
HD = 128
QPK = 2
NEW_TOK = 512


rope_base = 1000000.0
norm_eps = 1e-06
masked_score = -1e30


def row_norm(values, weight_gain):
    squares = jnp.mean(values * values, axis=-1, keepdims=True)
    return values * lax.rsqrt(squares + norm_eps) * weight_gain


def rotate(values, positions):
    half_width = values.shape[-1] // 2
    frequency = jnp.exp(
        jnp.arange(half_width, dtype=jnp.float32) * (-2.0 * math.log(rope_base) / values.shape[-1])
    )
    angle = positions.astype(jnp.float32)[:, None] * frequency[None, :]
    bcast_shape = (angle.shape[0],) + (1,) * (values.ndim - 2) + (half_width,)
    cosine = jnp.cos(angle).reshape(bcast_shape)
    sine_wave = jnp.sin(angle).reshape(bcast_shape)
    first_half = values[..., :half_width]
    second_half = values[..., half_width:]
    return jnp.concatenate(
        [
            first_half * cosine - second_half * sine_wave,
            second_half * cosine + first_half * sine_wave,
        ],
        axis=-1,
    )


def prepare(projected, positions, q_gain, k_gain):
    row_count = projected.shape[0]
    queries = projected[:, : QPK * HD].reshape(row_count, QPK, HD)
    key_part = projected[:, QPK * HD : QPK * HD + HD]
    value_part = projected[:, QPK * HD + HD : QPK * HD + 2 * HD]
    queries = (
        rotate(row_norm(queries, q_gain), positions)
        .astype(jnp.bfloat16)
        .reshape(row_count, QPK * HD)
    )
    key_part = rotate(row_norm(key_part, k_gain), positions).astype(jnp.bfloat16)
    value_part = value_part.astype(jnp.bfloat16)
    return (queries, key_part, value_part)


def update(carried, scores, values):
    running_top, running_sum, running_acc = carried
    new_top = jnp.maximum(running_top, jnp.max(scores, axis=-1))
    weights = jnp.exp(scores - new_top[..., None])
    factor = jnp.exp(running_top - new_top)
    new_sum = running_sum * factor + jnp.sum(weights, axis=-1)
    product = jnp.einsum(
        "hrs,hsd->hrd", weights.astype(jnp.bfloat16), values, preferred_element_type=jnp.float32
    )
    return (new_top, new_sum, running_acc * factor[..., None] + product)


def attend_one(queries, key_new, value_new, length, pages, k_pool, v_pool):
    heads_here = k_pool.shape[1]
    block_len = k_pool.shape[2]
    new_count = key_new.shape[0]
    row_total = new_count * QPK
    query_rows = (
        queries.reshape(new_count, heads_here, QPK, HD)
        .transpose(1, 0, 2, 3)
        .reshape(heads_here, row_total, HD)
    )
    step_pages = min(pages.shape[0], max(1, 1024 // block_len))
    span_keys = step_pages * block_len
    scale_factor = 1.0 / math.sqrt(HD)

    def one_turn(turn_index, carried):
        chosen = lax.dynamic_slice_in_dim(pages, turn_index * step_pages, step_pages)
        key_block = k_pool[chosen].transpose(1, 0, 2, 3).reshape(heads_here, span_keys, HD)
        value_block = v_pool[chosen].transpose(1, 0, 2, 3).reshape(heads_here, span_keys, HD)
        scores = (
            jnp.einsum("hrd,hsd->hrs", query_rows, key_block, preferred_element_type=jnp.float32)
            * scale_factor
        )
        placed = turn_index * span_keys + jnp.arange(span_keys, dtype=jnp.int32)
        scores = jnp.where(placed[None, None, :] < length, scores, masked_score)
        return update(carried, scores, value_block)

    start_state = (
        jnp.full((heads_here, row_total), masked_score, jnp.float32),
        jnp.zeros((heads_here, row_total), jnp.float32),
        jnp.zeros((heads_here, row_total, HD), jnp.float32),
    )
    turn_count = (length + span_keys - 1) // span_keys
    carried = lax.fori_loop(jnp.int32(0), turn_count, one_turn, start_state)
    new_keys = key_new.reshape(new_count, heads_here, HD).transpose(1, 0, 2)
    new_values = value_new.reshape(new_count, heads_here, HD).transpose(1, 0, 2)
    scores = (
        jnp.einsum("hrd,hsd->hrs", query_rows, new_keys, preferred_element_type=jnp.float32)
        * scale_factor
    )
    causal = (
        jnp.arange(row_total, dtype=jnp.int32)[:, None] // QPK
        >= jnp.arange(new_count, dtype=jnp.int32)[None, :]
    )
    scores = jnp.where(causal[None], scores, masked_score)
    top_row, sum_row, acc_row = update(carried, scores, new_values)
    result = acc_row / sum_row[..., None]
    return (
        result.reshape(heads_here, new_count, QPK, HD)
        .transpose(1, 0, 2, 3)
        .reshape(new_count, heads_here * QPK * HD)
    )


def attend_group(queries, key_rows, value_rows, cache_len, block_table, k_pool, v_pool):
    outputs = []
    for request in range(cache_len.shape[0]):
        row_start = request * NEW_TOK
        row_stop = row_start + NEW_TOK
        outputs.append(
            attend_one(
                queries[row_start:row_stop],
                key_rows[row_start:row_stop],
                value_rows[row_start:row_stop],
                cache_len[request],
                block_table[request],
                k_pool,
                v_pool,
            )
        )
    return jnp.concatenate(outputs, axis=0)


PAGES_STEP = 8


def flash_kernel(
    lens_ref, table_ref, q_ref, kn_ref, vn_ref, key_hbm, value_hbm, out_ref,
    key_buf, value_buf, copy_sem, top_sc, sum_sc, acc_sc,
):
    request = pl.program_id(0)
    length = lens_ref[request]
    rows = q_ref.shape[0]
    block_len = key_buf.shape[2]
    span = PAGES_STEP * block_len
    table_width = table_ref.shape[0] // pl.num_programs(0)
    blocks = (length + block_len - 1) // block_len
    turns = (length + span - 1) // span
    scale_factor = 1.0 / math.sqrt(HD)

    top_sc[...] = jnp.full(top_sc.shape, masked_score, jnp.float32)
    sum_sc[...] = jnp.zeros(sum_sc.shape, jnp.float32)
    acc_sc[...] = jnp.zeros(acc_sc.shape, jnp.float32)

    def page_copies(turn, slot):
        result = []
        for slot_page in range(PAGES_STEP):
            chosen = jnp.minimum(turn * PAGES_STEP + slot_page, jnp.maximum(blocks - 1, 0))
            page = table_ref[request * table_width + chosen]
            result.append(
                pltpu.make_async_copy(
                    key_hbm.at[page], key_buf.at[slot, slot_page], copy_sem.at[0, slot, slot_page]
                )
            )
            result.append(
                pltpu.make_async_copy(
                    value_hbm.at[page], value_buf.at[slot, slot_page], copy_sem.at[1, slot, slot_page]
                )
            )
        return result

    def absorb(keys, values, keep):
        for a in range(QPK):
            query = q_ref[:, a * HD : (a + 1) * HD]
            scores = (
                lax.dot_general(
                    query, keys, (((1,), (1,)), ((), ())), preferred_element_type=jnp.float32
                )
                * scale_factor
            )
            if keep is not None:
                scores = jnp.where(keep, scores, masked_score)
            running_top = top_sc[a]
            new_top = jnp.maximum(running_top, jnp.max(scores, axis=1, keepdims=True))
            weights = jnp.exp(scores - new_top)
            factor = jnp.exp(running_top - new_top)
            sum_sc[a] = sum_sc[a] * factor + jnp.sum(weights, axis=1, keepdims=True)
            product = jnp.dot(
                weights.astype(jnp.bfloat16), values, preferred_element_type=jnp.float32
            )
            acc_sc[a] = acc_sc[a] * factor + product
            top_sc[a] = new_top

    @pl.when(turns > 0)
    def _():
        for copy in page_copies(0, 0):
            copy.start()

    def one_turn(turn, carried):
        slot = turn % 2

        @pl.when(turn + 1 < turns)
        def _():
            for copy in page_copies(turn + 1, 1 - slot):
                copy.start()

        for copy in page_copies(turn, slot):
            copy.wait()
        keys = key_buf[slot].reshape(span, HD)
        values = value_buf[slot].reshape(span, HD)
        whole = (turn + 1) * span <= length

        @pl.when(whole)
        def _():
            absorb(keys, values, None)

        @pl.when(jnp.logical_not(whole))
        def _():
            placed = turn * span + lax.broadcasted_iota(jnp.int32, (1, span), 1)
            absorb(keys, values, placed < length)

        return carried

    lax.fori_loop(0, turns, one_turn, 0)
    causal = lax.broadcasted_iota(jnp.int32, (rows, rows), 0) >= lax.broadcasted_iota(
        jnp.int32, (rows, rows), 1
    )
    absorb(kn_ref[...], vn_ref[...], causal)
    for a in range(QPK):
        out_ref[:, a * HD : (a + 1) * HD] = (acc_sc[a] / sum_sc[a]).astype(out_ref.dtype)


def flash_attend(queries, key_rows, value_rows, cache_len, block_table, k_pool, v_pool):
    requests, table_width = block_table.shape
    pages_here, _, block_len, _ = k_pool.shape
    key_pages = k_pool.reshape(pages_here, block_len, HD)
    value_pages = v_pool.reshape(pages_here, block_len, HD)
    rows = queries.shape[0] // requests

    def row_spec(width):
        return pl.BlockSpec((rows, width), lambda request, lens_ref, table_ref: (request, 0))

    grid_spec = pltpu.PrefetchScalarGridSpec(
        num_scalar_prefetch=2,
        grid=(requests,),
        in_specs=[row_spec(QPK * HD), row_spec(HD), row_spec(HD)]
        + [pl.BlockSpec(memory_space=pl.ANY)] * 2,
        out_specs=row_spec(QPK * HD),
        scratch_shapes=[
            pltpu.VMEM((2, PAGES_STEP, block_len, HD), jnp.bfloat16),
            pltpu.VMEM((2, PAGES_STEP, block_len, HD), jnp.bfloat16),
            pltpu.SemaphoreType.DMA((2, 2, PAGES_STEP)),
            pltpu.VMEM((QPK, rows, 1), jnp.float32),
            pltpu.VMEM((QPK, rows, 1), jnp.float32),
            pltpu.VMEM((QPK, rows, HD), jnp.float32),
        ],
    )
    return pl.pallas_call(
        flash_kernel,
        grid_spec=grid_spec,
        out_shape=jax.ShapeDtypeStruct((queries.shape[0], QPK * HD), jnp.bfloat16),
        compiler_params=pltpu.CompilerParams(dimension_semantics=("arbitrary",)),
    )(cache_len, block_table.reshape(-1), queries, key_rows, value_rows, key_pages, value_pages)


def lengths_of(row_ids, cache_len):
    owners = row_ids // NEW_TOK
    matches = owners[:, None] == jnp.arange(cache_len.shape[0], dtype=jnp.int32)[None, :]
    return jnp.sum(jnp.where(matches, cache_len[None, :], 0), axis=1) + row_ids % NEW_TOK


def add_rows(left_side, weight_piece):
    return jnp.dot(left_side, weight_piece, preferred_element_type=jnp.float32)


def gather_columns(piece):
    req_count = lax.axis_size("req")
    copies = jnp.broadcast_to(piece[None], (req_count,) + piece.shape)
    return lax.all_to_all(copies, "req", 0, 0, tiled=True).reshape(-1, piece.shape[1])


def on_device(hidden_in, norm_gain, q_gain, k_gain, w_proj, cache_len, block_table, k_pool, v_pool):
    normed = row_norm(hidden_in.astype(jnp.float32), norm_gain).astype(jnp.bfloat16)
    split = QPK * HD + 2 * HD
    attend_columns = gather_columns(w_proj[:, :split])
    gate_columns = gather_columns(w_proj[:, split:])
    group_rows = lax.all_gather(normed, "head", axis=0, tiled=True)
    projected = add_rows(group_rows, attend_columns)
    row_ids = jnp.arange(group_rows.shape[0], dtype=jnp.int32)
    positions = lengths_of(row_ids, cache_len)
    queries, key_rows, value_rows = prepare(projected, positions, q_gain, k_gain)
    attention = flash_attend(
        queries, key_rows, value_rows, cache_len, block_table, k_pool, v_pool
    )
    gate_rows = add_rows(group_rows, gate_columns)
    gated = (attention.astype(jnp.float32) * jax.nn.sigmoid(gate_rows)).astype(jnp.bfloat16)
    return lax.all_to_all(gated, "head", split_axis=0, concat_axis=1, tiled=True)


def solution(mesh):
    in_specs = (
        P(("req", "head"), None),
        P(),
        P(),
        P(),
        P("req", "head"),
        P("req"),
        P("req", None),
        P("req", "head", None, None),
        P("req", "head", None, None),
    )
    out_specs = P(("req", "head"), None)
    return jax.shard_map(
        on_device, mesh=mesh, in_specs=in_specs, out_specs=out_specs, check_vma=False
    )
```

```python
import math

import jax
import jax.numpy as jnp
from jax import lax
from jax.experimental import pallas as pl
from jax.experimental.pallas import tpu as pltpu
from jax.sharding import PartitionSpec as P

KVH = 8
HD = 128
QPK = 2
NEW_TOK = 512


rope_base = 1000000.0
norm_eps = 1e-06
masked_score = -1e30


def row_norm(values, weight_gain):
    squares = jnp.mean(values * values, axis=-1, keepdims=True)
    return values * lax.rsqrt(squares + norm_eps) * weight_gain


def rotate(values, positions):
    half_width = values.shape[-1] // 2
    frequency = jnp.exp(
        jnp.arange(half_width, dtype=jnp.float32) * (-2.0 * math.log(rope_base) / values.shape[-1])
    )
    angle = positions.astype(jnp.float32)[:, None] * frequency[None, :]
    bcast_shape = (angle.shape[0],) + (1,) * (values.ndim - 2) + (half_width,)
    cosine = jnp.cos(angle).reshape(bcast_shape)
    sine_wave = jnp.sin(angle).reshape(bcast_shape)
    first_half = values[..., :half_width]
    second_half = values[..., half_width:]
    return jnp.concatenate(
        [
            first_half * cosine - second_half * sine_wave,
            second_half * cosine + first_half * sine_wave,
        ],
        axis=-1,
    )


def prepare(projected, positions, q_gain, k_gain):
    row_count = projected.shape[0]
    queries = projected[:, : QPK * HD].reshape(row_count, QPK, HD)
    key_part = projected[:, QPK * HD : QPK * HD + HD]
    value_part = projected[:, QPK * HD + HD : QPK * HD + 2 * HD]
    queries = (
        rotate(row_norm(queries, q_gain), positions)
        .astype(jnp.bfloat16)
        .reshape(row_count, QPK * HD)
    )
    key_part = rotate(row_norm(key_part, k_gain), positions).astype(jnp.bfloat16)
    value_part = value_part.astype(jnp.bfloat16)
    return (queries, key_part, value_part)


def update(carried, scores, values):
    running_top, running_sum, running_acc = carried
    new_top = jnp.maximum(running_top, jnp.max(scores, axis=-1))
    weights = jnp.exp(scores - new_top[..., None])
    factor = jnp.exp(running_top - new_top)
    new_sum = running_sum * factor + jnp.sum(weights, axis=-1)
    product = jnp.einsum(
        "hrs,hsd->hrd", weights.astype(jnp.bfloat16), values, preferred_element_type=jnp.float32
    )
    return (new_top, new_sum, running_acc * factor[..., None] + product)


def attend_one(queries, key_new, value_new, length, pages, k_pool, v_pool):
    heads_here = k_pool.shape[1]
    block_len = k_pool.shape[2]
    new_count = key_new.shape[0]
    row_total = new_count * QPK
    query_rows = (
        queries.reshape(new_count, heads_here, QPK, HD)
        .transpose(1, 0, 2, 3)
        .reshape(heads_here, row_total, HD)
    )
    step_pages = min(pages.shape[0], max(1, 1024 // block_len))
    span_keys = step_pages * block_len
    scale_factor = 1.0 / math.sqrt(HD)

    def one_turn(turn_index, carried):
        chosen = lax.dynamic_slice_in_dim(pages, turn_index * step_pages, step_pages)
        key_block = k_pool[chosen].transpose(1, 0, 2, 3).reshape(heads_here, span_keys, HD)
        value_block = v_pool[chosen].transpose(1, 0, 2, 3).reshape(heads_here, span_keys, HD)
        scores = (
            jnp.einsum("hrd,hsd->hrs", query_rows, key_block, preferred_element_type=jnp.float32)
            * scale_factor
        )
        placed = turn_index * span_keys + jnp.arange(span_keys, dtype=jnp.int32)
        scores = jnp.where(placed[None, None, :] < length, scores, masked_score)
        return update(carried, scores, value_block)

    start_state = (
        jnp.full((heads_here, row_total), masked_score, jnp.float32),
        jnp.zeros((heads_here, row_total), jnp.float32),
        jnp.zeros((heads_here, row_total, HD), jnp.float32),
    )
    turn_count = (length + span_keys - 1) // span_keys
    carried = lax.fori_loop(jnp.int32(0), turn_count, one_turn, start_state)
    new_keys = key_new.reshape(new_count, heads_here, HD).transpose(1, 0, 2)
    new_values = value_new.reshape(new_count, heads_here, HD).transpose(1, 0, 2)
    scores = (
        jnp.einsum("hrd,hsd->hrs", query_rows, new_keys, preferred_element_type=jnp.float32)
        * scale_factor
    )
    causal = (
        jnp.arange(row_total, dtype=jnp.int32)[:, None] // QPK
        >= jnp.arange(new_count, dtype=jnp.int32)[None, :]
    )
    scores = jnp.where(causal[None], scores, masked_score)
    top_row, sum_row, acc_row = update(carried, scores, new_values)
    result = acc_row / sum_row[..., None]
    return (
        result.reshape(heads_here, new_count, QPK, HD)
        .transpose(1, 0, 2, 3)
        .reshape(new_count, heads_here * QPK * HD)
    )


def attend_group(queries, key_rows, value_rows, cache_len, block_table, k_pool, v_pool):
    outputs = []
    for request in range(cache_len.shape[0]):
        row_start = request * NEW_TOK
        row_stop = row_start + NEW_TOK
        outputs.append(
            attend_one(
                queries[row_start:row_stop],
                key_rows[row_start:row_stop],
                value_rows[row_start:row_stop],
                cache_len[request],
                block_table[request],
                k_pool,
                v_pool,
            )
        )
    return jnp.concatenate(outputs, axis=0)


PAGES_STEP = 8
LANES = 128


def flash_kernel(
    lens_ref, table_ref, q_ref, kn_ref, vn_ref, key_hbm, value_hbm, out_ref,
    key_buf, value_buf, copy_sem, top_sc, sum_sc, acc_sc,
):
    request = pl.program_id(0)
    length = lens_ref[request]
    rows = q_ref.shape[0]
    block_len = key_buf.shape[2]
    span = PAGES_STEP * block_len
    table_width = table_ref.shape[0] // pl.num_programs(0)
    blocks = (length + block_len - 1) // block_len
    turns = (length + span - 1) // span
    log2_scale = math.log2(math.e) / math.sqrt(HD)

    top_sc[...] = jnp.full(top_sc.shape, masked_score, jnp.float32)
    sum_sc[...] = jnp.zeros(sum_sc.shape, jnp.float32)
    acc_sc[...] = jnp.zeros(acc_sc.shape, jnp.float32)

    def page_copies(turn, slot):
        result = []
        for slot_page in range(PAGES_STEP):
            chosen = jnp.minimum(turn * PAGES_STEP + slot_page, jnp.maximum(blocks - 1, 0))
            page = table_ref[request * table_width + chosen]
            result.append(
                pltpu.make_async_copy(
                    key_hbm.at[page], key_buf.at[slot, slot_page], copy_sem.at[0, slot, slot_page]
                )
            )
            result.append(
                pltpu.make_async_copy(
                    value_hbm.at[page], value_buf.at[slot, slot_page], copy_sem.at[1, slot, slot_page]
                )
            )
        return result

    def absorb(keys, values, keep):
        for a in range(QPK):
            query = q_ref[:, a * HD : (a + 1) * HD]
            scores = (
                lax.dot_general(
                    query, keys, (((1,), (1,)), ((), ())), preferred_element_type=jnp.float32
                )
                * log2_scale
            )
            if keep is not None:
                scores = jnp.where(keep, scores, masked_score)
            running_top = top_sc[a]
            new_top = jnp.maximum(running_top, jnp.max(scores, axis=1, keepdims=True))
            weights = jnp.exp2(scores - new_top[:, :1])
            factor = jnp.exp2(running_top - new_top)
            sum_sc[a] = sum_sc[a] * factor + jnp.sum(weights, axis=1, keepdims=True)
            product = jnp.dot(
                weights.astype(jnp.bfloat16), values, preferred_element_type=jnp.float32
            )
            acc_sc[a] = acc_sc[a] * factor[:, :1] + product
            top_sc[a] = new_top

    @pl.when(turns > 0)
    def _():
        for copy in page_copies(0, 0):
            copy.start()

    def one_turn(turn, carried):
        slot = turn % 2

        @pl.when(turn + 1 < turns)
        def _():
            for copy in page_copies(turn + 1, 1 - slot):
                copy.start()

        for copy in page_copies(turn, slot):
            copy.wait()
        keys = key_buf[slot].reshape(span, HD)
        values = value_buf[slot].reshape(span, HD)
        whole = (turn + 1) * span <= length

        @pl.when(whole)
        def _():
            absorb(keys, values, None)

        @pl.when(jnp.logical_not(whole))
        def _():
            placed = turn * span + lax.broadcasted_iota(jnp.int32, (1, span), 1)
            absorb(keys, values, placed < length)

        return carried

    lax.fori_loop(0, turns, one_turn, 0)
    causal = lax.broadcasted_iota(jnp.int32, (rows, rows), 0) >= lax.broadcasted_iota(
        jnp.int32, (rows, rows), 1
    )
    absorb(kn_ref[...], vn_ref[...], causal)
    for a in range(QPK):
        out_ref[:, a * HD : (a + 1) * HD] = (acc_sc[a] / sum_sc[a][:, :1]).astype(out_ref.dtype)


def flash_attend(queries, key_rows, value_rows, cache_len, block_table, k_pool, v_pool):
    requests, table_width = block_table.shape
    pages_here, _, block_len, _ = k_pool.shape
    key_pages = k_pool.reshape(pages_here, block_len, HD)
    value_pages = v_pool.reshape(pages_here, block_len, HD)
    rows = queries.shape[0] // requests

    def row_spec(width):
        return pl.BlockSpec((rows, width), lambda request, lens_ref, table_ref: (request, 0))

    grid_spec = pltpu.PrefetchScalarGridSpec(
        num_scalar_prefetch=2,
        grid=(requests,),
        in_specs=[row_spec(QPK * HD), row_spec(HD), row_spec(HD)]
        + [pl.BlockSpec(memory_space=pl.ANY)] * 2,
        out_specs=row_spec(QPK * HD),
        scratch_shapes=[
            pltpu.VMEM((2, PAGES_STEP, block_len, HD), jnp.bfloat16),
            pltpu.VMEM((2, PAGES_STEP, block_len, HD), jnp.bfloat16),
            pltpu.SemaphoreType.DMA((2, 2, PAGES_STEP)),
            pltpu.VMEM((QPK, rows, LANES), jnp.float32),
            pltpu.VMEM((QPK, rows, LANES), jnp.float32),
            pltpu.VMEM((QPK, rows, HD), jnp.float32),
        ],
    )
    return pl.pallas_call(
        flash_kernel,
        grid_spec=grid_spec,
        out_shape=jax.ShapeDtypeStruct((queries.shape[0], QPK * HD), jnp.bfloat16),
        compiler_params=pltpu.CompilerParams(dimension_semantics=("arbitrary",)),
    )(cache_len, block_table.reshape(-1), queries, key_rows, value_rows, key_pages, value_pages)


def lengths_of(row_ids, cache_len):
    owners = row_ids // NEW_TOK
    matches = owners[:, None] == jnp.arange(cache_len.shape[0], dtype=jnp.int32)[None, :]
    return jnp.sum(jnp.where(matches, cache_len[None, :], 0), axis=1) + row_ids % NEW_TOK


def add_rows(left_side, weight_piece):
    return jnp.dot(left_side, weight_piece, preferred_element_type=jnp.float32)


def gather_columns(piece):
    req_count = lax.axis_size("req")
    copies = jnp.broadcast_to(piece[None], (req_count,) + piece.shape)
    return lax.all_to_all(copies, "req", 0, 0, tiled=True).reshape(-1, piece.shape[1])


def on_device(hidden_in, norm_gain, q_gain, k_gain, w_proj, cache_len, block_table, k_pool, v_pool):
    normed = row_norm(hidden_in.astype(jnp.float32), norm_gain).astype(jnp.bfloat16)
    split = QPK * HD + 2 * HD
    attend_columns = gather_columns(w_proj[:, :split])
    gate_columns = lax.all_gather(w_proj[:, split:], "req", axis=0, tiled=True)
    group_rows = lax.all_gather(normed, "head", axis=0, tiled=True)
    projected = add_rows(group_rows, attend_columns)
    row_ids = jnp.arange(group_rows.shape[0], dtype=jnp.int32)
    positions = lengths_of(row_ids, cache_len)
    queries, key_rows, value_rows = prepare(projected, positions, q_gain, k_gain)
    attention = flash_attend(
        queries, key_rows, value_rows, cache_len, block_table, k_pool, v_pool
    )
    gate_rows = add_rows(group_rows, gate_columns)
    gated = (attention.astype(jnp.float32) * jax.nn.sigmoid(gate_rows)).astype(jnp.bfloat16)
    return lax.all_to_all(gated, "head", split_axis=0, concat_axis=1, tiled=True)


def solution(mesh):
    in_specs = (
        P(("req", "head"), None),
        P(),
        P(),
        P(),
        P("req", "head"),
        P("req"),
        P("req", None),
        P("req", "head", None, None),
        P("req", "head", None, None),
    )
    out_specs = P(("req", "head"), None)
    return jax.shard_map(
        on_device, mesh=mesh, in_specs=in_specs, out_specs=out_specs, check_vma=False
    )
```

```python
import math

import jax
import jax.numpy as jnp
from jax import lax
from jax.experimental import pallas as pl
from jax.experimental.pallas import tpu as pltpu
from jax.sharding import PartitionSpec as P

KVH = 8
HD = 128
QPK = 2
NEW_TOK = 512


rope_base = 1000000.0
norm_eps = 1e-06
masked_score = -1e30


def row_norm(values, weight_gain):
    squares = jnp.mean(values * values, axis=-1, keepdims=True)
    return values * lax.rsqrt(squares + norm_eps) * weight_gain


def rotate(values, positions):
    half_width = values.shape[-1] // 2
    frequency = jnp.exp(
        jnp.arange(half_width, dtype=jnp.float32) * (-2.0 * math.log(rope_base) / values.shape[-1])
    )
    angle = positions.astype(jnp.float32)[:, None] * frequency[None, :]
    bcast_shape = (angle.shape[0],) + (1,) * (values.ndim - 2) + (half_width,)
    cosine = jnp.cos(angle).reshape(bcast_shape)
    sine_wave = jnp.sin(angle).reshape(bcast_shape)
    first_half = values[..., :half_width]
    second_half = values[..., half_width:]
    return jnp.concatenate(
        [
            first_half * cosine - second_half * sine_wave,
            second_half * cosine + first_half * sine_wave,
        ],
        axis=-1,
    )


def prepare(projected, positions, q_gain, k_gain):
    row_count = projected.shape[0]
    queries = projected[:, : QPK * HD].reshape(row_count, QPK, HD)
    key_part = projected[:, QPK * HD : QPK * HD + HD]
    value_part = projected[:, QPK * HD + HD : QPK * HD + 2 * HD]
    queries = (
        rotate(row_norm(queries, q_gain), positions)
        .astype(jnp.bfloat16)
        .reshape(row_count, QPK * HD)
    )
    key_part = rotate(row_norm(key_part, k_gain), positions).astype(jnp.bfloat16)
    value_part = value_part.astype(jnp.bfloat16)
    return (queries, key_part, value_part)


def update(carried, scores, values):
    running_top, running_sum, running_acc = carried
    new_top = jnp.maximum(running_top, jnp.max(scores, axis=-1))
    weights = jnp.exp(scores - new_top[..., None])
    factor = jnp.exp(running_top - new_top)
    new_sum = running_sum * factor + jnp.sum(weights, axis=-1)
    product = jnp.einsum(
        "hrs,hsd->hrd", weights.astype(jnp.bfloat16), values, preferred_element_type=jnp.float32
    )
    return (new_top, new_sum, running_acc * factor[..., None] + product)


def attend_one(queries, key_new, value_new, length, pages, k_pool, v_pool):
    heads_here = k_pool.shape[1]
    block_len = k_pool.shape[2]
    new_count = key_new.shape[0]
    row_total = new_count * QPK
    query_rows = (
        queries.reshape(new_count, heads_here, QPK, HD)
        .transpose(1, 0, 2, 3)
        .reshape(heads_here, row_total, HD)
    )
    step_pages = min(pages.shape[0], max(1, 1024 // block_len))
    span_keys = step_pages * block_len
    scale_factor = 1.0 / math.sqrt(HD)

    def one_turn(turn_index, carried):
        chosen = lax.dynamic_slice_in_dim(pages, turn_index * step_pages, step_pages)
        key_block = k_pool[chosen].transpose(1, 0, 2, 3).reshape(heads_here, span_keys, HD)
        value_block = v_pool[chosen].transpose(1, 0, 2, 3).reshape(heads_here, span_keys, HD)
        scores = (
            jnp.einsum("hrd,hsd->hrs", query_rows, key_block, preferred_element_type=jnp.float32)
            * scale_factor
        )
        placed = turn_index * span_keys + jnp.arange(span_keys, dtype=jnp.int32)
        scores = jnp.where(placed[None, None, :] < length, scores, masked_score)
        return update(carried, scores, value_block)

    start_state = (
        jnp.full((heads_here, row_total), masked_score, jnp.float32),
        jnp.zeros((heads_here, row_total), jnp.float32),
        jnp.zeros((heads_here, row_total, HD), jnp.float32),
    )
    turn_count = (length + span_keys - 1) // span_keys
    carried = lax.fori_loop(jnp.int32(0), turn_count, one_turn, start_state)
    new_keys = key_new.reshape(new_count, heads_here, HD).transpose(1, 0, 2)
    new_values = value_new.reshape(new_count, heads_here, HD).transpose(1, 0, 2)
    scores = (
        jnp.einsum("hrd,hsd->hrs", query_rows, new_keys, preferred_element_type=jnp.float32)
        * scale_factor
    )
    causal = (
        jnp.arange(row_total, dtype=jnp.int32)[:, None] // QPK
        >= jnp.arange(new_count, dtype=jnp.int32)[None, :]
    )
    scores = jnp.where(causal[None], scores, masked_score)
    top_row, sum_row, acc_row = update(carried, scores, new_values)
    result = acc_row / sum_row[..., None]
    return (
        result.reshape(heads_here, new_count, QPK, HD)
        .transpose(1, 0, 2, 3)
        .reshape(new_count, heads_here * QPK * HD)
    )


def attend_group(queries, key_rows, value_rows, cache_len, block_table, k_pool, v_pool):
    outputs = []
    for request in range(cache_len.shape[0]):
        row_start = request * NEW_TOK
        row_stop = row_start + NEW_TOK
        outputs.append(
            attend_one(
                queries[row_start:row_stop],
                key_rows[row_start:row_stop],
                value_rows[row_start:row_stop],
                cache_len[request],
                block_table[request],
                k_pool,
                v_pool,
            )
        )
    return jnp.concatenate(outputs, axis=0)


PAGES_STEP = 8
LANES = 128


def flash_kernel(
    lens_ref, table_ref, q_ref, kn_ref, vn_ref, key_hbm, value_hbm, out_ref,
    key_buf, value_buf, copy_sem, top_sc, sum_sc, acc_sc,
):
    request = pl.program_id(0)
    length = lens_ref[request]
    rows = q_ref.shape[0]
    block_len = key_buf.shape[2]
    span = PAGES_STEP * block_len
    table_width = table_ref.shape[0] // pl.num_programs(0)
    blocks = (length + block_len - 1) // block_len
    turns = (length + span - 1) // span
    log2_scale = math.log2(math.e) / math.sqrt(HD)

    top_sc[...] = jnp.full(top_sc.shape, masked_score, jnp.float32)
    sum_sc[...] = jnp.zeros(sum_sc.shape, jnp.float32)
    acc_sc[...] = jnp.zeros(acc_sc.shape, jnp.float32)

    def page_copies(turn, slot):
        result = []
        for slot_page in range(PAGES_STEP):
            chosen = jnp.minimum(turn * PAGES_STEP + slot_page, jnp.maximum(blocks - 1, 0))
            page = table_ref[request * table_width + chosen]
            result.append(
                pltpu.make_async_copy(
                    key_hbm.at[page], key_buf.at[slot, slot_page], copy_sem.at[0, slot, slot_page]
                )
            )
            result.append(
                pltpu.make_async_copy(
                    value_hbm.at[page], value_buf.at[slot, slot_page], copy_sem.at[1, slot, slot_page]
                )
            )
        return result

    def absorb(keys, values, keep):
        for a in range(QPK):
            query = q_ref[:, a * HD : (a + 1) * HD]
            scores = (
                lax.dot_general(
                    query, keys, (((1,), (1,)), ((), ())), preferred_element_type=jnp.float32
                )
                * log2_scale
            )
            if keep is not None:
                scores = jnp.where(keep, scores, masked_score)
            running_top = top_sc[a]
            new_top = jnp.maximum(running_top, jnp.max(scores, axis=1, keepdims=True))
            weights = jnp.exp2(scores - new_top[:, :1])
            factor = jnp.exp2(running_top - new_top)
            sum_sc[a] = sum_sc[a] * factor + jnp.sum(weights, axis=1, keepdims=True)
            product = jnp.dot(
                weights.astype(jnp.bfloat16), values, preferred_element_type=jnp.float32
            )
            acc_sc[a] = acc_sc[a] * factor[:, :1] + product
            top_sc[a] = new_top

    @pl.when(turns > 0)
    def _():
        for copy in page_copies(0, 0):
            copy.start()

    def one_turn(turn, carried):
        slot = turn % 2

        @pl.when(turn + 1 < turns)
        def _():
            for copy in page_copies(turn + 1, 1 - slot):
                copy.start()

        for copy in page_copies(turn, slot):
            copy.wait()
        keys = key_buf[slot].reshape(span, HD)
        values = value_buf[slot].reshape(span, HD)
        whole = (turn + 1) * span <= length

        @pl.when(whole)
        def _():
            absorb(keys, values, None)

        @pl.when(jnp.logical_not(whole))
        def _():
            placed = turn * span + lax.broadcasted_iota(jnp.int32, (1, span), 1)
            absorb(keys, values, placed < length)

        return carried

    lax.fori_loop(0, turns, one_turn, 0)
    causal = lax.broadcasted_iota(jnp.int32, (rows, rows), 0) >= lax.broadcasted_iota(
        jnp.int32, (rows, rows), 1
    )
    absorb(kn_ref[...], vn_ref[...], causal)
    for a in range(QPK):
        out_ref[:, a * HD : (a + 1) * HD] = (acc_sc[a] / sum_sc[a][:, :1]).astype(out_ref.dtype)


def flash_attend(queries, key_rows, value_rows, cache_len, block_table, k_pool, v_pool):
    requests, table_width = block_table.shape
    pages_here, _, block_len, _ = k_pool.shape
    key_pages = k_pool.reshape(pages_here, block_len, HD)
    value_pages = v_pool.reshape(pages_here, block_len, HD)
    rows = queries.shape[0] // requests

    def row_spec(width):
        return pl.BlockSpec((rows, width), lambda request, lens_ref, table_ref: (request, 0))

    grid_spec = pltpu.PrefetchScalarGridSpec(
        num_scalar_prefetch=2,
        grid=(requests,),
        in_specs=[row_spec(QPK * HD), row_spec(HD), row_spec(HD)]
        + [pl.BlockSpec(memory_space=pl.ANY)] * 2,
        out_specs=row_spec(QPK * HD),
        scratch_shapes=[
            pltpu.VMEM((2, PAGES_STEP, block_len, HD), jnp.bfloat16),
            pltpu.VMEM((2, PAGES_STEP, block_len, HD), jnp.bfloat16),
            pltpu.SemaphoreType.DMA((2, 2, PAGES_STEP)),
            pltpu.VMEM((QPK, rows, LANES), jnp.float32),
            pltpu.VMEM((QPK, rows, LANES), jnp.float32),
            pltpu.VMEM((QPK, rows, HD), jnp.float32),
        ],
    )
    return pl.pallas_call(
        flash_kernel,
        grid_spec=grid_spec,
        out_shape=jax.ShapeDtypeStruct((queries.shape[0], QPK * HD), jnp.bfloat16),
        compiler_params=pltpu.CompilerParams(dimension_semantics=("arbitrary",)),
    )(cache_len, block_table.reshape(-1), queries, key_rows, value_rows, key_pages, value_pages)


def project_kernel(x_ref, w_ref, cos_ref, sin_ref, qg_ref, kg_ref, q_out, k_out, v_out):
    projected = jnp.dot(x_ref[...], w_ref[...], preferred_element_type=jnp.float32)
    cosine = cos_ref[...]
    sine = sin_ref[...]

    def norm_rotate(part, gain):
        squares = jnp.mean(part * part, axis=1, keepdims=True)
        normed = part * lax.rsqrt(squares + norm_eps) * gain
        return normed * cosine + pltpu.roll(normed, HD // 2, 1) * sine

    for a in range(QPK):
        q_out[:, a * HD : (a + 1) * HD] = norm_rotate(
            projected[:, a * HD : (a + 1) * HD], qg_ref[...]
        ).astype(q_out.dtype)
    k_out[...] = norm_rotate(
        projected[:, QPK * HD : QPK * HD + HD], kg_ref[...]
    ).astype(k_out.dtype)
    v_out[...] = projected[:, QPK * HD + HD : QPK * HD + 2 * HD].astype(v_out.dtype)


def project_prepare(group_rows, attend_columns, positions, q_gain, k_gain):
    row_count, width = group_rows.shape
    half_width = HD // 2
    frequency = jnp.exp(
        jnp.arange(half_width, dtype=jnp.float32) * (-2.0 * math.log(rope_base) / HD)
    )
    angle = positions.astype(jnp.float32)[:, None] * frequency[None, :]
    cosine = jnp.cos(angle)
    sine_wave = jnp.sin(angle)
    cos_full = jnp.concatenate([cosine, cosine], axis=1)
    sin_signed = jnp.concatenate([-sine_wave, sine_wave], axis=1)
    block_rows = 256
    columns = attend_columns.shape[1]

    def rows_of(cols):
        return pl.BlockSpec((block_rows, cols), lambda i: (i, 0))

    whole = lambda shape: pl.BlockSpec(shape, lambda i: (0, 0))
    return pl.pallas_call(
        project_kernel,
        grid=(row_count // block_rows,),
        in_specs=[
            rows_of(width),
            whole((width, columns)),
            rows_of(HD),
            rows_of(HD),
            whole((1, HD)),
            whole((1, HD)),
        ],
        out_specs=[rows_of(QPK * HD), rows_of(HD), rows_of(HD)],
        out_shape=[
            jax.ShapeDtypeStruct((row_count, QPK * HD), jnp.bfloat16),
            jax.ShapeDtypeStruct((row_count, HD), jnp.bfloat16),
            jax.ShapeDtypeStruct((row_count, HD), jnp.bfloat16),
        ],
    )(group_rows, attend_columns, cos_full, sin_signed, q_gain.reshape(1, HD), k_gain.reshape(1, HD))


def lengths_of(row_ids, cache_len):
    owners = row_ids // NEW_TOK
    matches = owners[:, None] == jnp.arange(cache_len.shape[0], dtype=jnp.int32)[None, :]
    return jnp.sum(jnp.where(matches, cache_len[None, :], 0), axis=1) + row_ids % NEW_TOK


def add_rows(left_side, weight_piece):
    return jnp.dot(left_side, weight_piece, preferred_element_type=jnp.float32)


def gather_columns(piece):
    req_count = lax.axis_size("req")
    copies = jnp.broadcast_to(piece[None], (req_count,) + piece.shape)
    return lax.all_to_all(copies, "req", 0, 0, tiled=True).reshape(-1, piece.shape[1])


def on_device(hidden_in, norm_gain, q_gain, k_gain, w_proj, cache_len, block_table, k_pool, v_pool):
    normed = row_norm(hidden_in.astype(jnp.float32), norm_gain).astype(jnp.bfloat16)
    split = QPK * HD + 2 * HD
    attend_columns = gather_columns(w_proj[:, :split])
    gate_columns = lax.all_gather(w_proj[:, split:], "req", axis=0, tiled=True)
    group_rows = lax.all_gather(normed, "head", axis=0, tiled=True)
    row_ids = jnp.arange(group_rows.shape[0], dtype=jnp.int32)
    positions = lengths_of(row_ids, cache_len)
    queries, key_rows, value_rows = project_prepare(
        group_rows, attend_columns, positions, q_gain, k_gain
    )
    attention = flash_attend(
        queries, key_rows, value_rows, cache_len, block_table, k_pool, v_pool
    )
    gate_rows = add_rows(group_rows, gate_columns)
    gated = (attention.astype(jnp.float32) * jax.nn.sigmoid(gate_rows)).astype(jnp.bfloat16)
    return lax.all_to_all(gated, "head", split_axis=0, concat_axis=1, tiled=True)


def solution(mesh):
    in_specs = (
        P(("req", "head"), None),
        P(),
        P(),
        P(),
        P("req", "head"),
        P("req"),
        P("req", None),
        P("req", "head", None, None),
        P("req", "head", None, None),
    )
    out_specs = P(("req", "head"), None)
    return jax.shard_map(
        on_device, mesh=mesh, in_specs=in_specs, out_specs=out_specs, check_vma=False
    )
```

```python
import functools
import math

import jax
import jax.numpy as jnp
from jax import lax
from jax.experimental import pallas as pl
from jax.experimental.pallas import tpu as pltpu
from jax.sharding import PartitionSpec as P

KVH = 8
HD = 128
QPK = 2
NEW_TOK = 512


rope_base = 1000000.0
norm_eps = 1e-06
masked_score = -1e30


def row_norm(values, weight_gain):
    squares = jnp.mean(values * values, axis=-1, keepdims=True)
    return values * lax.rsqrt(squares + norm_eps) * weight_gain


def rotate(values, positions):
    half_width = values.shape[-1] // 2
    frequency = jnp.exp(
        jnp.arange(half_width, dtype=jnp.float32) * (-2.0 * math.log(rope_base) / values.shape[-1])
    )
    angle = positions.astype(jnp.float32)[:, None] * frequency[None, :]
    bcast_shape = (angle.shape[0],) + (1,) * (values.ndim - 2) + (half_width,)
    cosine = jnp.cos(angle).reshape(bcast_shape)
    sine_wave = jnp.sin(angle).reshape(bcast_shape)
    first_half = values[..., :half_width]
    second_half = values[..., half_width:]
    return jnp.concatenate(
        [
            first_half * cosine - second_half * sine_wave,
            second_half * cosine + first_half * sine_wave,
        ],
        axis=-1,
    )


def prepare(projected, positions, q_gain, k_gain):
    row_count = projected.shape[0]
    queries = projected[:, : QPK * HD].reshape(row_count, QPK, HD)
    key_part = projected[:, QPK * HD : QPK * HD + HD]
    value_part = projected[:, QPK * HD + HD : QPK * HD + 2 * HD]
    queries = (
        rotate(row_norm(queries, q_gain), positions)
        .astype(jnp.bfloat16)
        .reshape(row_count, QPK * HD)
    )
    key_part = rotate(row_norm(key_part, k_gain), positions).astype(jnp.bfloat16)
    value_part = value_part.astype(jnp.bfloat16)
    return (queries, key_part, value_part)


def update(carried, scores, values):
    running_top, running_sum, running_acc = carried
    new_top = jnp.maximum(running_top, jnp.max(scores, axis=-1))
    weights = jnp.exp(scores - new_top[..., None])
    factor = jnp.exp(running_top - new_top)
    new_sum = running_sum * factor + jnp.sum(weights, axis=-1)
    product = jnp.einsum(
        "hrs,hsd->hrd", weights.astype(jnp.bfloat16), values, preferred_element_type=jnp.float32
    )
    return (new_top, new_sum, running_acc * factor[..., None] + product)


def attend_one(queries, key_new, value_new, length, pages, k_pool, v_pool):
    heads_here = k_pool.shape[1]
    block_len = k_pool.shape[2]
    new_count = key_new.shape[0]
    row_total = new_count * QPK
    query_rows = (
        queries.reshape(new_count, heads_here, QPK, HD)
        .transpose(1, 0, 2, 3)
        .reshape(heads_here, row_total, HD)
    )
    step_pages = min(pages.shape[0], max(1, 1024 // block_len))
    span_keys = step_pages * block_len
    scale_factor = 1.0 / math.sqrt(HD)

    def one_turn(turn_index, carried):
        chosen = lax.dynamic_slice_in_dim(pages, turn_index * step_pages, step_pages)
        key_block = k_pool[chosen].transpose(1, 0, 2, 3).reshape(heads_here, span_keys, HD)
        value_block = v_pool[chosen].transpose(1, 0, 2, 3).reshape(heads_here, span_keys, HD)
        scores = (
            jnp.einsum("hrd,hsd->hrs", query_rows, key_block, preferred_element_type=jnp.float32)
            * scale_factor
        )
        placed = turn_index * span_keys + jnp.arange(span_keys, dtype=jnp.int32)
        scores = jnp.where(placed[None, None, :] < length, scores, masked_score)
        return update(carried, scores, value_block)

    start_state = (
        jnp.full((heads_here, row_total), masked_score, jnp.float32),
        jnp.zeros((heads_here, row_total), jnp.float32),
        jnp.zeros((heads_here, row_total, HD), jnp.float32),
    )
    turn_count = (length + span_keys - 1) // span_keys
    carried = lax.fori_loop(jnp.int32(0), turn_count, one_turn, start_state)
    new_keys = key_new.reshape(new_count, heads_here, HD).transpose(1, 0, 2)
    new_values = value_new.reshape(new_count, heads_here, HD).transpose(1, 0, 2)
    scores = (
        jnp.einsum("hrd,hsd->hrs", query_rows, new_keys, preferred_element_type=jnp.float32)
        * scale_factor
    )
    causal = (
        jnp.arange(row_total, dtype=jnp.int32)[:, None] // QPK
        >= jnp.arange(new_count, dtype=jnp.int32)[None, :]
    )
    scores = jnp.where(causal[None], scores, masked_score)
    top_row, sum_row, acc_row = update(carried, scores, new_values)
    result = acc_row / sum_row[..., None]
    return (
        result.reshape(heads_here, new_count, QPK, HD)
        .transpose(1, 0, 2, 3)
        .reshape(new_count, heads_here * QPK * HD)
    )


def attend_group(queries, key_rows, value_rows, cache_len, block_table, k_pool, v_pool):
    outputs = []
    for request in range(cache_len.shape[0]):
        row_start = request * NEW_TOK
        row_stop = row_start + NEW_TOK
        outputs.append(
            attend_one(
                queries[row_start:row_stop],
                key_rows[row_start:row_stop],
                value_rows[row_start:row_stop],
                cache_len[request],
                block_table[request],
                k_pool,
                v_pool,
            )
        )
    return jnp.concatenate(outputs, axis=0)


PAGES_STEP = 8
LANES = 128


def flash_kernel(
    piece, offset, lens_ref, table_ref, q_ref, kn_ref, vn_ref, key_hbm, value_hbm, out_ref,
    key_buf, value_buf, copy_sem, top_sc, sum_sc, acc_sc,
):
    request = pl.program_id(0)
    length = lens_ref[request]
    rows = q_ref.shape[0]
    block_len = key_buf.shape[2]
    span = PAGES_STEP * block_len
    table_width = table_ref.shape[0] // pl.num_programs(0)
    blocks = (length + block_len - 1) // block_len
    turns = (length + span - 1) // span
    log2_scale = math.log2(math.e) / math.sqrt(HD)

    top_sc[...] = jnp.full(top_sc.shape, masked_score, jnp.float32)
    sum_sc[...] = jnp.zeros(sum_sc.shape, jnp.float32)
    acc_sc[...] = jnp.zeros(acc_sc.shape, jnp.float32)

    def page_copies(turn, slot):
        result = []
        for slot_page in range(PAGES_STEP):
            chosen = jnp.minimum(turn * PAGES_STEP + slot_page, jnp.maximum(blocks - 1, 0))
            page = table_ref[request * table_width + chosen]
            result.append(
                pltpu.make_async_copy(
                    key_hbm.at[page], key_buf.at[slot, slot_page], copy_sem.at[0, slot, slot_page]
                )
            )
            result.append(
                pltpu.make_async_copy(
                    value_hbm.at[page], value_buf.at[slot, slot_page], copy_sem.at[1, slot, slot_page]
                )
            )
        return result

    def absorb(keys, values, keep):
        for a in range(QPK):
            query = q_ref[:, a * HD : (a + 1) * HD]
            scores = (
                lax.dot_general(
                    query, keys, (((1,), (1,)), ((), ())), preferred_element_type=jnp.float32
                )
                * log2_scale
            )
            if keep is not None:
                scores = jnp.where(keep, scores, masked_score)
            running_top = top_sc[a]
            new_top = jnp.maximum(running_top, jnp.max(scores, axis=1, keepdims=True))
            weights = jnp.exp2(scores - new_top[:, :1])
            factor = jnp.exp2(running_top - new_top)
            sum_sc[a] = sum_sc[a] * factor + jnp.sum(weights, axis=1, keepdims=True)
            product = jnp.dot(
                weights.astype(jnp.bfloat16), values, preferred_element_type=jnp.float32
            )
            acc_sc[a] = acc_sc[a] * factor[:, :1] + product
            top_sc[a] = new_top

    @pl.when(turns > 0)
    def _():
        for copy in page_copies(0, 0):
            copy.start()

    def one_turn(turn, carried):
        slot = turn % 2

        @pl.when(turn + 1 < turns)
        def _():
            for copy in page_copies(turn + 1, 1 - slot):
                copy.start()

        for copy in page_copies(turn, slot):
            copy.wait()
        keys = key_buf[slot].reshape(span, HD)
        values = value_buf[slot].reshape(span, HD)
        whole = (turn + 1) * span <= length

        @pl.when(whole)
        def _():
            absorb(keys, values, None)

        @pl.when(jnp.logical_not(whole))
        def _():
            placed = turn * span + lax.broadcasted_iota(jnp.int32, (1, span), 1)
            absorb(keys, values, placed < length)

        return carried

    lax.fori_loop(0, turns, one_turn, 0)
    new_count = kn_ref.shape[0]
    row_index = lax.broadcasted_iota(jnp.int32, (rows, new_count), 0)
    row_token = row_index // piece * (2 * piece) + offset + row_index % piece
    causal = row_token >= lax.broadcasted_iota(jnp.int32, (rows, new_count), 1)
    absorb(kn_ref[...], vn_ref[...], causal)
    for a in range(QPK):
        out_ref[:, a * HD : (a + 1) * HD] = (acc_sc[a] / sum_sc[a][:, :1]).astype(out_ref.dtype)


def flash_attend(queries, key_rows, value_rows, cache_len, block_table, k_pool, v_pool, piece, offset):
    requests, table_width = block_table.shape
    pages_here, _, block_len, _ = k_pool.shape
    key_pages = k_pool.reshape(pages_here, block_len, HD)
    value_pages = v_pool.reshape(pages_here, block_len, HD)
    rows = queries.shape[0] // requests
    new_count = key_rows.shape[0] // requests

    def row_spec(width, count=rows):
        return pl.BlockSpec((count, width), lambda request, lens_ref, table_ref: (request, 0))

    grid_spec = pltpu.PrefetchScalarGridSpec(
        num_scalar_prefetch=2,
        grid=(requests,),
        in_specs=[row_spec(QPK * HD), row_spec(HD, new_count), row_spec(HD, new_count)]
        + [pl.BlockSpec(memory_space=pl.ANY)] * 2,
        out_specs=row_spec(QPK * HD),
        scratch_shapes=[
            pltpu.VMEM((2, PAGES_STEP, block_len, HD), jnp.bfloat16),
            pltpu.VMEM((2, PAGES_STEP, block_len, HD), jnp.bfloat16),
            pltpu.SemaphoreType.DMA((2, 2, PAGES_STEP)),
            pltpu.VMEM((QPK, rows, LANES), jnp.float32),
            pltpu.VMEM((QPK, rows, LANES), jnp.float32),
            pltpu.VMEM((QPK, rows, HD), jnp.float32),
        ],
    )
    return pl.pallas_call(
        functools.partial(flash_kernel, piece, offset),
        grid_spec=grid_spec,
        out_shape=jax.ShapeDtypeStruct((queries.shape[0], QPK * HD), jnp.bfloat16),
        compiler_params=pltpu.CompilerParams(dimension_semantics=("arbitrary",)),
    )(cache_len, block_table.reshape(-1), queries, key_rows, value_rows, key_pages, value_pages)


def project_kernel(x_ref, w_ref, cos_ref, sin_ref, qg_ref, kg_ref, q_out, k_out, v_out):
    projected = jnp.dot(x_ref[...], w_ref[...], preferred_element_type=jnp.float32)
    cosine = cos_ref[...]
    sine = sin_ref[...]

    def norm_rotate(part, gain):
        squares = jnp.mean(part * part, axis=1, keepdims=True)
        normed = part * lax.rsqrt(squares + norm_eps) * gain
        return normed * cosine + pltpu.roll(normed, HD // 2, 1) * sine

    for a in range(QPK):
        q_out[:, a * HD : (a + 1) * HD] = norm_rotate(
            projected[:, a * HD : (a + 1) * HD], qg_ref[...]
        ).astype(q_out.dtype)
    k_out[...] = norm_rotate(
        projected[:, QPK * HD : QPK * HD + HD], kg_ref[...]
    ).astype(k_out.dtype)
    v_out[...] = projected[:, QPK * HD + HD : QPK * HD + 2 * HD].astype(v_out.dtype)


def project_prepare(group_rows, attend_columns, positions, q_gain, k_gain):
    row_count, width = group_rows.shape
    half_width = HD // 2
    frequency = jnp.exp(
        jnp.arange(half_width, dtype=jnp.float32) * (-2.0 * math.log(rope_base) / HD)
    )
    angle = positions.astype(jnp.float32)[:, None] * frequency[None, :]
    cosine = jnp.cos(angle)
    sine_wave = jnp.sin(angle)
    cos_full = jnp.concatenate([cosine, cosine], axis=1)
    sin_signed = jnp.concatenate([-sine_wave, sine_wave], axis=1)
    block_rows = 256
    columns = attend_columns.shape[1]

    def rows_of(cols):
        return pl.BlockSpec((block_rows, cols), lambda i: (i, 0))

    whole = lambda shape: pl.BlockSpec(shape, lambda i: (0, 0))
    return pl.pallas_call(
        project_kernel,
        grid=(row_count // block_rows,),
        in_specs=[
            rows_of(width),
            whole((width, columns)),
            rows_of(HD),
            rows_of(HD),
            whole((1, HD)),
            whole((1, HD)),
        ],
        out_specs=[rows_of(QPK * HD), rows_of(HD), rows_of(HD)],
        out_shape=[
            jax.ShapeDtypeStruct((row_count, QPK * HD), jnp.bfloat16),
            jax.ShapeDtypeStruct((row_count, HD), jnp.bfloat16),
            jax.ShapeDtypeStruct((row_count, HD), jnp.bfloat16),
        ],
    )(group_rows, attend_columns, cos_full, sin_signed, q_gain.reshape(1, HD), k_gain.reshape(1, HD))


def lengths_of(row_ids, cache_len):
    owners = row_ids // NEW_TOK
    matches = owners[:, None] == jnp.arange(cache_len.shape[0], dtype=jnp.int32)[None, :]
    return jnp.sum(jnp.where(matches, cache_len[None, :], 0), axis=1) + row_ids % NEW_TOK


def add_rows(left_side, weight_piece):
    return jnp.dot(left_side, weight_piece, preferred_element_type=jnp.float32)


def gather_columns(piece):
    req_count = lax.axis_size("req")
    copies = jnp.broadcast_to(piece[None], (req_count,) + piece.shape)
    return lax.all_to_all(copies, "req", 0, 0, tiled=True).reshape(-1, piece.shape[1])


def on_device(hidden_in, norm_gain, q_gain, k_gain, w_proj, cache_len, block_table, k_pool, v_pool):
    normed = row_norm(hidden_in.astype(jnp.float32), norm_gain).astype(jnp.bfloat16)
    split = QPK * HD + 2 * HD
    attend_columns = gather_columns(w_proj[:, :split])
    gate_columns = lax.all_gather(w_proj[:, split:], "req", axis=0, tiled=True)
    group_rows = lax.all_gather(normed, "head", axis=0, tiled=True)
    row_ids = jnp.arange(group_rows.shape[0], dtype=jnp.int32)
    positions = lengths_of(row_ids, cache_len)
    queries, key_rows, value_rows = project_prepare(
        group_rows, attend_columns, positions, q_gain, k_gain
    )
    owners = lax.axis_size("head")
    parts = 2
    piece = hidden_in.shape[0] // parts

    def pick(values, part):
        return values.reshape(owners, parts, piece, -1)[:, part].reshape(owners * piece, -1)

    returned = []
    for part in range(parts):
        attention = flash_attend(
            pick(queries, part), key_rows, value_rows, cache_len, block_table, k_pool, v_pool,
            piece, part * piece,
        )
        gate_rows = add_rows(pick(group_rows, part), gate_columns)
        gated = (attention.astype(jnp.float32) * jax.nn.sigmoid(gate_rows)).astype(jnp.bfloat16)
        returned.append(lax.all_to_all(gated, "head", split_axis=0, concat_axis=1, tiled=True))
    return jnp.concatenate(returned, axis=0)


def solution(mesh):
    in_specs = (
        P(("req", "head"), None),
        P(),
        P(),
        P(),
        P("req", "head"),
        P("req"),
        P("req", None),
        P("req", "head", None, None),
        P("req", "head", None, None),
    )
    out_specs = P(("req", "head"), None)
    return jax.shard_map(
        on_device, mesh=mesh, in_specs=in_specs, out_specs=out_specs, check_vma=False
    )
```

```python
import math

import jax
import jax.numpy as jnp
from jax import lax
from jax.experimental import pallas as pl
from jax.experimental.pallas import tpu as pltpu
from jax.sharding import PartitionSpec as P

KVH = 8
HD = 128
QPK = 2
NEW_TOK = 512


rope_base = 1000000.0
norm_eps = 1e-06
masked_score = -1e30


def row_norm(values, weight_gain):
    squares = jnp.mean(values * values, axis=-1, keepdims=True)
    return values * lax.rsqrt(squares + norm_eps) * weight_gain


def rotate(values, positions):
    half_width = values.shape[-1] // 2
    frequency = jnp.exp(
        jnp.arange(half_width, dtype=jnp.float32) * (-2.0 * math.log(rope_base) / values.shape[-1])
    )
    angle = positions.astype(jnp.float32)[:, None] * frequency[None, :]
    bcast_shape = (angle.shape[0],) + (1,) * (values.ndim - 2) + (half_width,)
    cosine = jnp.cos(angle).reshape(bcast_shape)
    sine_wave = jnp.sin(angle).reshape(bcast_shape)
    first_half = values[..., :half_width]
    second_half = values[..., half_width:]
    return jnp.concatenate(
        [
            first_half * cosine - second_half * sine_wave,
            second_half * cosine + first_half * sine_wave,
        ],
        axis=-1,
    )


def prepare(projected, positions, q_gain, k_gain):
    row_count = projected.shape[0]
    queries = projected[:, : QPK * HD].reshape(row_count, QPK, HD)
    key_part = projected[:, QPK * HD : QPK * HD + HD]
    value_part = projected[:, QPK * HD + HD : QPK * HD + 2 * HD]
    queries = (
        rotate(row_norm(queries, q_gain), positions)
        .astype(jnp.bfloat16)
        .reshape(row_count, QPK * HD)
    )
    key_part = rotate(row_norm(key_part, k_gain), positions).astype(jnp.bfloat16)
    value_part = value_part.astype(jnp.bfloat16)
    return (queries, key_part, value_part)


def update(carried, scores, values):
    running_top, running_sum, running_acc = carried
    new_top = jnp.maximum(running_top, jnp.max(scores, axis=-1))
    weights = jnp.exp(scores - new_top[..., None])
    factor = jnp.exp(running_top - new_top)
    new_sum = running_sum * factor + jnp.sum(weights, axis=-1)
    product = jnp.einsum(
        "hrs,hsd->hrd", weights.astype(jnp.bfloat16), values, preferred_element_type=jnp.float32
    )
    return (new_top, new_sum, running_acc * factor[..., None] + product)


def attend_one(queries, key_new, value_new, length, pages, k_pool, v_pool):
    heads_here = k_pool.shape[1]
    block_len = k_pool.shape[2]
    new_count = key_new.shape[0]
    row_total = new_count * QPK
    query_rows = (
        queries.reshape(new_count, heads_here, QPK, HD)
        .transpose(1, 0, 2, 3)
        .reshape(heads_here, row_total, HD)
    )
    step_pages = min(pages.shape[0], max(1, 1024 // block_len))
    span_keys = step_pages * block_len
    scale_factor = 1.0 / math.sqrt(HD)

    def one_turn(turn_index, carried):
        chosen = lax.dynamic_slice_in_dim(pages, turn_index * step_pages, step_pages)
        key_block = k_pool[chosen].transpose(1, 0, 2, 3).reshape(heads_here, span_keys, HD)
        value_block = v_pool[chosen].transpose(1, 0, 2, 3).reshape(heads_here, span_keys, HD)
        scores = (
            jnp.einsum("hrd,hsd->hrs", query_rows, key_block, preferred_element_type=jnp.float32)
            * scale_factor
        )
        placed = turn_index * span_keys + jnp.arange(span_keys, dtype=jnp.int32)
        scores = jnp.where(placed[None, None, :] < length, scores, masked_score)
        return update(carried, scores, value_block)

    start_state = (
        jnp.full((heads_here, row_total), masked_score, jnp.float32),
        jnp.zeros((heads_here, row_total), jnp.float32),
        jnp.zeros((heads_here, row_total, HD), jnp.float32),
    )
    turn_count = (length + span_keys - 1) // span_keys
    carried = lax.fori_loop(jnp.int32(0), turn_count, one_turn, start_state)
    new_keys = key_new.reshape(new_count, heads_here, HD).transpose(1, 0, 2)
    new_values = value_new.reshape(new_count, heads_here, HD).transpose(1, 0, 2)
    scores = (
        jnp.einsum("hrd,hsd->hrs", query_rows, new_keys, preferred_element_type=jnp.float32)
        * scale_factor
    )
    causal = (
        jnp.arange(row_total, dtype=jnp.int32)[:, None] // QPK
        >= jnp.arange(new_count, dtype=jnp.int32)[None, :]
    )
    scores = jnp.where(causal[None], scores, masked_score)
    top_row, sum_row, acc_row = update(carried, scores, new_values)
    result = acc_row / sum_row[..., None]
    return (
        result.reshape(heads_here, new_count, QPK, HD)
        .transpose(1, 0, 2, 3)
        .reshape(new_count, heads_here * QPK * HD)
    )


def attend_group(queries, key_rows, value_rows, cache_len, block_table, k_pool, v_pool):
    outputs = []
    for request in range(cache_len.shape[0]):
        row_start = request * NEW_TOK
        row_stop = row_start + NEW_TOK
        outputs.append(
            attend_one(
                queries[row_start:row_stop],
                key_rows[row_start:row_stop],
                value_rows[row_start:row_stop],
                cache_len[request],
                block_table[request],
                k_pool,
                v_pool,
            )
        )
    return jnp.concatenate(outputs, axis=0)


PAGES_STEP = 32
LANES = 128


def flash_kernel(
    lens_ref, table_ref, q_ref, kn_ref, vn_ref, key_hbm, value_hbm, out_ref,
    key_buf, value_buf, copy_sem, top_sc, sum_sc, acc_sc,
):
    request = pl.program_id(0)
    length = lens_ref[request]
    rows = q_ref.shape[0]
    block_len = key_buf.shape[2]
    span = PAGES_STEP * block_len
    table_width = table_ref.shape[0] // pl.num_programs(0)
    blocks = (length + block_len - 1) // block_len
    turns = (length + span - 1) // span
    log2_scale = math.log2(math.e) / math.sqrt(HD)

    top_sc[...] = jnp.full(top_sc.shape, masked_score, jnp.float32)
    sum_sc[...] = jnp.zeros(sum_sc.shape, jnp.float32)
    acc_sc[...] = jnp.zeros(acc_sc.shape, jnp.float32)

    def page_copies(turn, slot):
        result = []
        for slot_page in range(PAGES_STEP):
            chosen = jnp.minimum(turn * PAGES_STEP + slot_page, jnp.maximum(blocks - 1, 0))
            page = table_ref[request * table_width + chosen]
            result.append(
                pltpu.make_async_copy(
                    key_hbm.at[page], key_buf.at[slot, slot_page], copy_sem.at[0, slot, slot_page]
                )
            )
            result.append(
                pltpu.make_async_copy(
                    value_hbm.at[page], value_buf.at[slot, slot_page], copy_sem.at[1, slot, slot_page]
                )
            )
        return result

    def absorb(keys, values, keep):
        for a in range(QPK):
            query = q_ref[:, a * HD : (a + 1) * HD]
            scores = (
                lax.dot_general(
                    query, keys, (((1,), (1,)), ((), ())), preferred_element_type=jnp.float32
                )
                * log2_scale
            )
            if keep is not None:
                scores = jnp.where(keep, scores, masked_score)
            running_top = top_sc[a]
            new_top = jnp.maximum(running_top, jnp.max(scores, axis=1, keepdims=True))
            weights = jnp.exp2(scores - new_top[:, :1])
            factor = jnp.exp2(running_top - new_top)
            sum_sc[a] = sum_sc[a] * factor + jnp.sum(weights, axis=1, keepdims=True)
            product = jnp.dot(
                weights.astype(jnp.bfloat16), values, preferred_element_type=jnp.float32
            )
            acc_sc[a] = acc_sc[a] * factor[:, :1] + product
            top_sc[a] = new_top

    @pl.when(turns > 0)
    def _():
        for copy in page_copies(0, 0):
            copy.start()

    def one_turn(turn, carried):
        slot = turn % 2

        @pl.when(turn + 1 < turns)
        def _():
            for copy in page_copies(turn + 1, 1 - slot):
                copy.start()

        for copy in page_copies(turn, slot):
            copy.wait()
        keys = key_buf[slot].reshape(span, HD)
        values = value_buf[slot].reshape(span, HD)
        whole = (turn + 1) * span <= length

        @pl.when(whole)
        def _():
            absorb(keys, values, None)

        @pl.when(jnp.logical_not(whole))
        def _():
            placed = turn * span + lax.broadcasted_iota(jnp.int32, (1, span), 1)
            absorb(keys, values, placed < length)

        return carried

    lax.fori_loop(0, turns, one_turn, 0)
    causal = lax.broadcasted_iota(jnp.int32, (rows, rows), 0) >= lax.broadcasted_iota(
        jnp.int32, (rows, rows), 1
    )
    absorb(kn_ref[...], vn_ref[...], causal)
    for a in range(QPK):
        out_ref[:, a * HD : (a + 1) * HD] = (acc_sc[a] / sum_sc[a][:, :1]).astype(out_ref.dtype)


def flash_attend(queries, key_rows, value_rows, cache_len, block_table, k_pool, v_pool):
    requests, table_width = block_table.shape
    pages_here, _, block_len, _ = k_pool.shape
    key_pages = k_pool.reshape(pages_here, block_len, HD)
    value_pages = v_pool.reshape(pages_here, block_len, HD)
    rows = queries.shape[0] // requests

    def row_spec(width):
        return pl.BlockSpec((rows, width), lambda request, lens_ref, table_ref: (request, 0))

    grid_spec = pltpu.PrefetchScalarGridSpec(
        num_scalar_prefetch=2,
        grid=(requests,),
        in_specs=[row_spec(QPK * HD), row_spec(HD), row_spec(HD)]
        + [pl.BlockSpec(memory_space=pl.ANY)] * 2,
        out_specs=row_spec(QPK * HD),
        scratch_shapes=[
            pltpu.VMEM((2, PAGES_STEP, block_len, HD), jnp.bfloat16),
            pltpu.VMEM((2, PAGES_STEP, block_len, HD), jnp.bfloat16),
            pltpu.SemaphoreType.DMA((2, 2, PAGES_STEP)),
            pltpu.VMEM((QPK, rows, LANES), jnp.float32),
            pltpu.VMEM((QPK, rows, LANES), jnp.float32),
            pltpu.VMEM((QPK, rows, HD), jnp.float32),
        ],
    )
    return pl.pallas_call(
        flash_kernel,
        grid_spec=grid_spec,
        out_shape=jax.ShapeDtypeStruct((queries.shape[0], QPK * HD), jnp.bfloat16),
        compiler_params=pltpu.CompilerParams(dimension_semantics=("arbitrary",)),
    )(cache_len, block_table.reshape(-1), queries, key_rows, value_rows, key_pages, value_pages)


def project_kernel(x_ref, w_ref, cos_ref, sin_ref, qg_ref, kg_ref, q_out, k_out, v_out):
    projected = jnp.dot(x_ref[...], w_ref[...], preferred_element_type=jnp.float32)
    cosine = cos_ref[...]
    sine = sin_ref[...]

    def norm_rotate(part, gain):
        squares = jnp.mean(part * part, axis=1, keepdims=True)
        normed = part * lax.rsqrt(squares + norm_eps) * gain
        return normed * cosine + pltpu.roll(normed, HD // 2, 1) * sine

    for a in range(QPK):
        q_out[:, a * HD : (a + 1) * HD] = norm_rotate(
            projected[:, a * HD : (a + 1) * HD], qg_ref[...]
        ).astype(q_out.dtype)
    k_out[...] = norm_rotate(
        projected[:, QPK * HD : QPK * HD + HD], kg_ref[...]
    ).astype(k_out.dtype)
    v_out[...] = projected[:, QPK * HD + HD : QPK * HD + 2 * HD].astype(v_out.dtype)


def project_prepare(group_rows, attend_columns, positions, q_gain, k_gain):
    row_count, width = group_rows.shape
    half_width = HD // 2
    frequency = jnp.exp(
        jnp.arange(half_width, dtype=jnp.float32) * (-2.0 * math.log(rope_base) / HD)
    )
    angle = positions.astype(jnp.float32)[:, None] * frequency[None, :]
    cosine = jnp.cos(angle)
    sine_wave = jnp.sin(angle)
    cos_full = jnp.concatenate([cosine, cosine], axis=1)
    sin_signed = jnp.concatenate([-sine_wave, sine_wave], axis=1)
    block_rows = 256
    columns = attend_columns.shape[1]

    def rows_of(cols):
        return pl.BlockSpec((block_rows, cols), lambda i: (i, 0))

    whole = lambda shape: pl.BlockSpec(shape, lambda i: (0, 0))
    return pl.pallas_call(
        project_kernel,
        grid=(row_count // block_rows,),
        in_specs=[
            rows_of(width),
            whole((width, columns)),
            rows_of(HD),
            rows_of(HD),
            whole((1, HD)),
            whole((1, HD)),
        ],
        out_specs=[rows_of(QPK * HD), rows_of(HD), rows_of(HD)],
        out_shape=[
            jax.ShapeDtypeStruct((row_count, QPK * HD), jnp.bfloat16),
            jax.ShapeDtypeStruct((row_count, HD), jnp.bfloat16),
            jax.ShapeDtypeStruct((row_count, HD), jnp.bfloat16),
        ],
    )(group_rows, attend_columns, cos_full, sin_signed, q_gain.reshape(1, HD), k_gain.reshape(1, HD))


def lengths_of(row_ids, cache_len):
    owners = row_ids // NEW_TOK
    matches = owners[:, None] == jnp.arange(cache_len.shape[0], dtype=jnp.int32)[None, :]
    return jnp.sum(jnp.where(matches, cache_len[None, :], 0), axis=1) + row_ids % NEW_TOK


def add_rows(left_side, weight_piece):
    return jnp.dot(left_side, weight_piece, preferred_element_type=jnp.float32)


def gather_columns(piece):
    req_count = lax.axis_size("req")
    copies = jnp.broadcast_to(piece[None], (req_count,) + piece.shape)
    return lax.all_to_all(copies, "req", 0, 0, tiled=True).reshape(-1, piece.shape[1])


def on_device(hidden_in, norm_gain, q_gain, k_gain, w_proj, cache_len, block_table, k_pool, v_pool):
    normed = row_norm(hidden_in.astype(jnp.float32), norm_gain).astype(jnp.bfloat16)
    split = QPK * HD + 2 * HD
    attend_columns = gather_columns(w_proj[:, :split])
    gate_columns = lax.all_gather(w_proj[:, split:], "req", axis=0, tiled=True)
    group_rows = lax.all_gather(normed, "head", axis=0, tiled=True)
    row_ids = jnp.arange(group_rows.shape[0], dtype=jnp.int32)
    positions = lengths_of(row_ids, cache_len)
    queries, key_rows, value_rows = project_prepare(
        group_rows, attend_columns, positions, q_gain, k_gain
    )
    attention = flash_attend(
        queries, key_rows, value_rows, cache_len, block_table, k_pool, v_pool
    )
    gate_rows = add_rows(group_rows, gate_columns)
    gated = (attention.astype(jnp.float32) * jax.nn.sigmoid(gate_rows)).astype(jnp.bfloat16)
    return lax.all_to_all(gated, "head", split_axis=0, concat_axis=1, tiled=True)


def solution(mesh):
    in_specs = (
        P(("req", "head"), None),
        P(),
        P(),
        P(),
        P("req", "head"),
        P("req"),
        P("req", None),
        P("req", "head", None, None),
        P("req", "head", None, None),
    )
    out_specs = P(("req", "head"), None)
    return jax.shard_map(
        on_device, mesh=mesh, in_specs=in_specs, out_specs=out_specs, check_vma=False
    )
```

```python
import math

import jax
import jax.numpy as jnp
from jax import lax
from jax.experimental import pallas as pl
from jax.experimental.pallas import tpu as pltpu
from jax.sharding import PartitionSpec as P

KVH = 8
HD = 128
QPK = 2
NEW_TOK = 512


rope_base = 1000000.0
norm_eps = 1e-06
masked_score = -1e30


def row_norm(values, weight_gain):
    squares = jnp.mean(values * values, axis=-1, keepdims=True)
    return values * lax.rsqrt(squares + norm_eps) * weight_gain


def rotate(values, positions):
    half_width = values.shape[-1] // 2
    frequency = jnp.exp(
        jnp.arange(half_width, dtype=jnp.float32) * (-2.0 * math.log(rope_base) / values.shape[-1])
    )
    angle = positions.astype(jnp.float32)[:, None] * frequency[None, :]
    bcast_shape = (angle.shape[0],) + (1,) * (values.ndim - 2) + (half_width,)
    cosine = jnp.cos(angle).reshape(bcast_shape)
    sine_wave = jnp.sin(angle).reshape(bcast_shape)
    first_half = values[..., :half_width]
    second_half = values[..., half_width:]
    return jnp.concatenate(
        [
            first_half * cosine - second_half * sine_wave,
            second_half * cosine + first_half * sine_wave,
        ],
        axis=-1,
    )


def prepare(projected, positions, q_gain, k_gain):
    row_count = projected.shape[0]
    queries = projected[:, : QPK * HD].reshape(row_count, QPK, HD)
    key_part = projected[:, QPK * HD : QPK * HD + HD]
    value_part = projected[:, QPK * HD + HD : QPK * HD + 2 * HD]
    queries = (
        rotate(row_norm(queries, q_gain), positions)
        .astype(jnp.bfloat16)
        .reshape(row_count, QPK * HD)
    )
    key_part = rotate(row_norm(key_part, k_gain), positions).astype(jnp.bfloat16)
    value_part = value_part.astype(jnp.bfloat16)
    return (queries, key_part, value_part)


def update(carried, scores, values):
    running_top, running_sum, running_acc = carried
    new_top = jnp.maximum(running_top, jnp.max(scores, axis=-1))
    weights = jnp.exp(scores - new_top[..., None])
    factor = jnp.exp(running_top - new_top)
    new_sum = running_sum * factor + jnp.sum(weights, axis=-1)
    product = jnp.einsum(
        "hrs,hsd->hrd", weights.astype(jnp.bfloat16), values, preferred_element_type=jnp.float32
    )
    return (new_top, new_sum, running_acc * factor[..., None] + product)


def attend_one(queries, key_new, value_new, length, pages, k_pool, v_pool):
    heads_here = k_pool.shape[1]
    block_len = k_pool.shape[2]
    new_count = key_new.shape[0]
    row_total = new_count * QPK
    query_rows = (
        queries.reshape(new_count, heads_here, QPK, HD)
        .transpose(1, 0, 2, 3)
        .reshape(heads_here, row_total, HD)
    )
    step_pages = min(pages.shape[0], max(1, 1024 // block_len))
    span_keys = step_pages * block_len
    scale_factor = 1.0 / math.sqrt(HD)

    def one_turn(turn_index, carried):
        chosen = lax.dynamic_slice_in_dim(pages, turn_index * step_pages, step_pages)
        key_block = k_pool[chosen].transpose(1, 0, 2, 3).reshape(heads_here, span_keys, HD)
        value_block = v_pool[chosen].transpose(1, 0, 2, 3).reshape(heads_here, span_keys, HD)
        scores = (
            jnp.einsum("hrd,hsd->hrs", query_rows, key_block, preferred_element_type=jnp.float32)
            * scale_factor
        )
        placed = turn_index * span_keys + jnp.arange(span_keys, dtype=jnp.int32)
        scores = jnp.where(placed[None, None, :] < length, scores, masked_score)
        return update(carried, scores, value_block)

    start_state = (
        jnp.full((heads_here, row_total), masked_score, jnp.float32),
        jnp.zeros((heads_here, row_total), jnp.float32),
        jnp.zeros((heads_here, row_total, HD), jnp.float32),
    )
    turn_count = (length + span_keys - 1) // span_keys
    carried = lax.fori_loop(jnp.int32(0), turn_count, one_turn, start_state)
    new_keys = key_new.reshape(new_count, heads_here, HD).transpose(1, 0, 2)
    new_values = value_new.reshape(new_count, heads_here, HD).transpose(1, 0, 2)
    scores = (
        jnp.einsum("hrd,hsd->hrs", query_rows, new_keys, preferred_element_type=jnp.float32)
        * scale_factor
    )
    causal = (
        jnp.arange(row_total, dtype=jnp.int32)[:, None] // QPK
        >= jnp.arange(new_count, dtype=jnp.int32)[None, :]
    )
    scores = jnp.where(causal[None], scores, masked_score)
    top_row, sum_row, acc_row = update(carried, scores, new_values)
    result = acc_row / sum_row[..., None]
    return (
        result.reshape(heads_here, new_count, QPK, HD)
        .transpose(1, 0, 2, 3)
        .reshape(new_count, heads_here * QPK * HD)
    )


def attend_group(queries, key_rows, value_rows, cache_len, block_table, k_pool, v_pool):
    outputs = []
    for request in range(cache_len.shape[0]):
        row_start = request * NEW_TOK
        row_stop = row_start + NEW_TOK
        outputs.append(
            attend_one(
                queries[row_start:row_stop],
                key_rows[row_start:row_stop],
                value_rows[row_start:row_stop],
                cache_len[request],
                block_table[request],
                k_pool,
                v_pool,
            )
        )
    return jnp.concatenate(outputs, axis=0)


PAGES_STEP = 16
LANES = 128


def flash_kernel(
    lens_ref, table_ref, q_ref, kn_ref, vn_ref, key_hbm, value_hbm, out_ref,
    key_buf, value_buf, copy_sem, top_sc, sum_sc, acc_sc,
):
    request = pl.program_id(0)
    length = lens_ref[request]
    rows = q_ref.shape[0]
    block_len = key_buf.shape[2]
    span = PAGES_STEP * block_len
    table_width = table_ref.shape[0] // pl.num_programs(0)
    blocks = (length + block_len - 1) // block_len
    turns = (length + span - 1) // span
    log2_scale = math.log2(math.e) / math.sqrt(HD)

    top_sc[...] = jnp.full(top_sc.shape, masked_score, jnp.float32)
    sum_sc[...] = jnp.zeros(sum_sc.shape, jnp.float32)
    acc_sc[...] = jnp.zeros(acc_sc.shape, jnp.float32)

    def page_copies(turn, slot):
        result = []
        for slot_page in range(PAGES_STEP):
            chosen = jnp.minimum(turn * PAGES_STEP + slot_page, jnp.maximum(blocks - 1, 0))
            page = table_ref[request * table_width + chosen]
            result.append(
                pltpu.make_async_copy(
                    key_hbm.at[page], key_buf.at[slot, slot_page], copy_sem.at[0, slot, slot_page]
                )
            )
            result.append(
                pltpu.make_async_copy(
                    value_hbm.at[page], value_buf.at[slot, slot_page], copy_sem.at[1, slot, slot_page]
                )
            )
        return result

    def absorb(keys, values, keep):
        for a in range(QPK):
            query = q_ref[:, a * HD : (a + 1) * HD]
            scores = (
                lax.dot_general(
                    query, keys, (((1,), (1,)), ((), ())), preferred_element_type=jnp.float32
                )
                * log2_scale
            )
            if keep is not None:
                scores = jnp.where(keep, scores, masked_score)
            running_top = top_sc[a]
            new_top = jnp.maximum(running_top, jnp.max(scores, axis=1, keepdims=True))
            weights = jnp.exp2(scores - new_top[:, :1])
            factor = jnp.exp2(running_top - new_top)
            sum_sc[a] = sum_sc[a] * factor + jnp.sum(weights, axis=1, keepdims=True)
            product = jnp.dot(
                weights.astype(jnp.bfloat16), values, preferred_element_type=jnp.float32
            )
            acc_sc[a] = acc_sc[a] * factor[:, :1] + product
            top_sc[a] = new_top

    @pl.when(turns > 0)
    def _():
        for copy in page_copies(0, 0):
            copy.start()

    def one_turn(turn, carried):
        slot = turn % 2

        @pl.when(turn + 1 < turns)
        def _():
            for copy in page_copies(turn + 1, 1 - slot):
                copy.start()

        for copy in page_copies(turn, slot):
            copy.wait()
        keys = key_buf[slot].reshape(span, HD)
        values = value_buf[slot].reshape(span, HD)
        whole = (turn + 1) * span <= length

        @pl.when(whole)
        def _():
            absorb(keys, values, None)

        @pl.when(jnp.logical_not(whole))
        def _():
            placed = turn * span + lax.broadcasted_iota(jnp.int32, (1, span), 1)
            absorb(keys, values, placed < length)

        return carried

    lax.fori_loop(0, turns, one_turn, 0)
    causal = lax.broadcasted_iota(jnp.int32, (rows, rows), 0) >= lax.broadcasted_iota(
        jnp.int32, (rows, rows), 1
    )
    absorb(kn_ref[...], vn_ref[...], causal)
    for a in range(QPK):
        out_ref[:, a * HD : (a + 1) * HD] = (acc_sc[a] / sum_sc[a][:, :1]).astype(out_ref.dtype)


def flash_attend(queries, key_rows, value_rows, cache_len, block_table, k_pool, v_pool):
    requests, table_width = block_table.shape
    pages_here, _, block_len, _ = k_pool.shape
    key_pages = k_pool.reshape(pages_here, block_len, HD)
    value_pages = v_pool.reshape(pages_here, block_len, HD)
    rows = queries.shape[0] // requests

    def row_spec(width):
        return pl.BlockSpec((rows, width), lambda request, lens_ref, table_ref: (request, 0))

    grid_spec = pltpu.PrefetchScalarGridSpec(
        num_scalar_prefetch=2,
        grid=(requests,),
        in_specs=[row_spec(QPK * HD), row_spec(HD), row_spec(HD)]
        + [pl.BlockSpec(memory_space=pl.ANY)] * 2,
        out_specs=row_spec(QPK * HD),
        scratch_shapes=[
            pltpu.VMEM((2, PAGES_STEP, block_len, HD), jnp.bfloat16),
            pltpu.VMEM((2, PAGES_STEP, block_len, HD), jnp.bfloat16),
            pltpu.SemaphoreType.DMA((2, 2, PAGES_STEP)),
            pltpu.VMEM((QPK, rows, LANES), jnp.float32),
            pltpu.VMEM((QPK, rows, LANES), jnp.float32),
            pltpu.VMEM((QPK, rows, HD), jnp.float32),
        ],
    )
    return pl.pallas_call(
        flash_kernel,
        grid_spec=grid_spec,
        out_shape=jax.ShapeDtypeStruct((queries.shape[0], QPK * HD), jnp.bfloat16),
        compiler_params=pltpu.CompilerParams(dimension_semantics=("arbitrary",)),
    )(cache_len, block_table.reshape(-1), queries, key_rows, value_rows, key_pages, value_pages)


def project_kernel(x_ref, w_ref, cos_ref, sin_ref, qg_ref, kg_ref, q_out, k_out, v_out):
    projected = jnp.dot(x_ref[...], w_ref[...], preferred_element_type=jnp.float32)
    cosine = cos_ref[...]
    sine = sin_ref[...]

    def norm_rotate(part, gain):
        squares = jnp.mean(part * part, axis=1, keepdims=True)
        normed = part * lax.rsqrt(squares + norm_eps) * gain
        return normed * cosine + pltpu.roll(normed, HD // 2, 1) * sine

    for a in range(QPK):
        q_out[:, a * HD : (a + 1) * HD] = norm_rotate(
            projected[:, a * HD : (a + 1) * HD], qg_ref[...]
        ).astype(q_out.dtype)
    k_out[...] = norm_rotate(
        projected[:, QPK * HD : QPK * HD + HD], kg_ref[...]
    ).astype(k_out.dtype)
    v_out[...] = projected[:, QPK * HD + HD : QPK * HD + 2 * HD].astype(v_out.dtype)


def project_prepare(group_rows, attend_columns, positions, q_gain, k_gain):
    row_count, width = group_rows.shape
    half_width = HD // 2
    frequency = jnp.exp(
        jnp.arange(half_width, dtype=jnp.float32) * (-2.0 * math.log(rope_base) / HD)
    )
    angle = positions.astype(jnp.float32)[:, None] * frequency[None, :]
    cosine = jnp.cos(angle)
    sine_wave = jnp.sin(angle)
    cos_full = jnp.concatenate([cosine, cosine], axis=1)
    sin_signed = jnp.concatenate([-sine_wave, sine_wave], axis=1)
    block_rows = 256
    columns = attend_columns.shape[1]

    def rows_of(cols):
        return pl.BlockSpec((block_rows, cols), lambda i: (i, 0))

    whole = lambda shape: pl.BlockSpec(shape, lambda i: (0, 0))
    return pl.pallas_call(
        project_kernel,
        grid=(row_count // block_rows,),
        in_specs=[
            rows_of(width),
            whole((width, columns)),
            rows_of(HD),
            rows_of(HD),
            whole((1, HD)),
            whole((1, HD)),
        ],
        out_specs=[rows_of(QPK * HD), rows_of(HD), rows_of(HD)],
        out_shape=[
            jax.ShapeDtypeStruct((row_count, QPK * HD), jnp.bfloat16),
            jax.ShapeDtypeStruct((row_count, HD), jnp.bfloat16),
            jax.ShapeDtypeStruct((row_count, HD), jnp.bfloat16),
        ],
    )(group_rows, attend_columns, cos_full, sin_signed, q_gain.reshape(1, HD), k_gain.reshape(1, HD))


def lengths_of(row_ids, cache_len):
    owners = row_ids // NEW_TOK
    matches = owners[:, None] == jnp.arange(cache_len.shape[0], dtype=jnp.int32)[None, :]
    return jnp.sum(jnp.where(matches, cache_len[None, :], 0), axis=1) + row_ids % NEW_TOK


def add_rows(left_side, weight_piece):
    return jnp.dot(left_side, weight_piece, preferred_element_type=jnp.float32)


def gather_columns(piece):
    req_count = lax.axis_size("req")
    copies = jnp.broadcast_to(piece[None], (req_count,) + piece.shape)
    return lax.all_to_all(copies, "req", 0, 0, tiled=True).reshape(-1, piece.shape[1])


def on_device(hidden_in, norm_gain, q_gain, k_gain, w_proj, cache_len, block_table, k_pool, v_pool):
    normed = row_norm(hidden_in.astype(jnp.float32), norm_gain).astype(jnp.bfloat16)
    split = QPK * HD + 2 * HD
    attend_columns = gather_columns(w_proj[:, :split])
    gate_columns = lax.all_gather(w_proj[:, split:], "req", axis=0, tiled=True)
    group_rows = lax.all_gather(normed, "head", axis=0, tiled=True)
    row_ids = jnp.arange(group_rows.shape[0], dtype=jnp.int32)
    positions = lengths_of(row_ids, cache_len)
    queries, key_rows, value_rows = project_prepare(
        group_rows, attend_columns, positions, q_gain, k_gain
    )
    attention = flash_attend(
        queries, key_rows, value_rows, cache_len, block_table, k_pool, v_pool
    )
    gate_rows = add_rows(group_rows, gate_columns)
    gated = (attention.astype(jnp.float32) * jax.nn.sigmoid(gate_rows)).astype(jnp.bfloat16)
    return lax.all_to_all(gated, "head", split_axis=0, concat_axis=1, tiled=True)


def solution(mesh):
    in_specs = (
        P(("req", "head"), None),
        P(),
        P(),
        P(),
        P("req", "head"),
        P("req"),
        P("req", None),
        P("req", "head", None, None),
        P("req", "head", None, None),
    )
    out_specs = P(("req", "head"), None)
    return jax.shard_map(
        on_device, mesh=mesh, in_specs=in_specs, out_specs=out_specs, check_vma=False
    )
```

```python
import math

import jax
import jax.numpy as jnp
from jax import lax
from jax.experimental import pallas as pl
from jax.experimental.pallas import tpu as pltpu
from jax.sharding import PartitionSpec as P

KVH = 8
HD = 128
QPK = 2
NEW_TOK = 512


rope_base = 1000000.0
norm_eps = 1e-06
masked_score = -1e30


def row_norm(values, weight_gain):
    squares = jnp.mean(values * values, axis=-1, keepdims=True)
    return values * lax.rsqrt(squares + norm_eps) * weight_gain


def rotate(values, positions):
    half_width = values.shape[-1] // 2
    frequency = jnp.exp(
        jnp.arange(half_width, dtype=jnp.float32) * (-2.0 * math.log(rope_base) / values.shape[-1])
    )
    angle = positions.astype(jnp.float32)[:, None] * frequency[None, :]
    bcast_shape = (angle.shape[0],) + (1,) * (values.ndim - 2) + (half_width,)
    cosine = jnp.cos(angle).reshape(bcast_shape)
    sine_wave = jnp.sin(angle).reshape(bcast_shape)
    first_half = values[..., :half_width]
    second_half = values[..., half_width:]
    return jnp.concatenate(
        [
            first_half * cosine - second_half * sine_wave,
            second_half * cosine + first_half * sine_wave,
        ],
        axis=-1,
    )


def prepare(projected, positions, q_gain, k_gain):
    row_count = projected.shape[0]
    queries = projected[:, : QPK * HD].reshape(row_count, QPK, HD)
    key_part = projected[:, QPK * HD : QPK * HD + HD]
    value_part = projected[:, QPK * HD + HD : QPK * HD + 2 * HD]
    queries = (
        rotate(row_norm(queries, q_gain), positions)
        .astype(jnp.bfloat16)
        .reshape(row_count, QPK * HD)
    )
    key_part = rotate(row_norm(key_part, k_gain), positions).astype(jnp.bfloat16)
    value_part = value_part.astype(jnp.bfloat16)
    return (queries, key_part, value_part)


def update(carried, scores, values):
    running_top, running_sum, running_acc = carried
    new_top = jnp.maximum(running_top, jnp.max(scores, axis=-1))
    weights = jnp.exp(scores - new_top[..., None])
    factor = jnp.exp(running_top - new_top)
    new_sum = running_sum * factor + jnp.sum(weights, axis=-1)
    product = jnp.einsum(
        "hrs,hsd->hrd", weights.astype(jnp.bfloat16), values, preferred_element_type=jnp.float32
    )
    return (new_top, new_sum, running_acc * factor[..., None] + product)


def attend_one(queries, key_new, value_new, length, pages, k_pool, v_pool):
    heads_here = k_pool.shape[1]
    block_len = k_pool.shape[2]
    new_count = key_new.shape[0]
    row_total = new_count * QPK
    query_rows = (
        queries.reshape(new_count, heads_here, QPK, HD)
        .transpose(1, 0, 2, 3)
        .reshape(heads_here, row_total, HD)
    )
    step_pages = min(pages.shape[0], max(1, 1024 // block_len))
    span_keys = step_pages * block_len
    scale_factor = 1.0 / math.sqrt(HD)

    def one_turn(turn_index, carried):
        chosen = lax.dynamic_slice_in_dim(pages, turn_index * step_pages, step_pages)
        key_block = k_pool[chosen].transpose(1, 0, 2, 3).reshape(heads_here, span_keys, HD)
        value_block = v_pool[chosen].transpose(1, 0, 2, 3).reshape(heads_here, span_keys, HD)
        scores = (
            jnp.einsum("hrd,hsd->hrs", query_rows, key_block, preferred_element_type=jnp.float32)
            * scale_factor
        )
        placed = turn_index * span_keys + jnp.arange(span_keys, dtype=jnp.int32)
        scores = jnp.where(placed[None, None, :] < length, scores, masked_score)
        return update(carried, scores, value_block)

    start_state = (
        jnp.full((heads_here, row_total), masked_score, jnp.float32),
        jnp.zeros((heads_here, row_total), jnp.float32),
        jnp.zeros((heads_here, row_total, HD), jnp.float32),
    )
    turn_count = (length + span_keys - 1) // span_keys
    carried = lax.fori_loop(jnp.int32(0), turn_count, one_turn, start_state)
    new_keys = key_new.reshape(new_count, heads_here, HD).transpose(1, 0, 2)
    new_values = value_new.reshape(new_count, heads_here, HD).transpose(1, 0, 2)
    scores = (
        jnp.einsum("hrd,hsd->hrs", query_rows, new_keys, preferred_element_type=jnp.float32)
        * scale_factor
    )
    causal = (
        jnp.arange(row_total, dtype=jnp.int32)[:, None] // QPK
        >= jnp.arange(new_count, dtype=jnp.int32)[None, :]
    )
    scores = jnp.where(causal[None], scores, masked_score)
    top_row, sum_row, acc_row = update(carried, scores, new_values)
    result = acc_row / sum_row[..., None]
    return (
        result.reshape(heads_here, new_count, QPK, HD)
        .transpose(1, 0, 2, 3)
        .reshape(new_count, heads_here * QPK * HD)
    )


def attend_group(queries, key_rows, value_rows, cache_len, block_table, k_pool, v_pool):
    outputs = []
    for request in range(cache_len.shape[0]):
        row_start = request * NEW_TOK
        row_stop = row_start + NEW_TOK
        outputs.append(
            attend_one(
                queries[row_start:row_stop],
                key_rows[row_start:row_stop],
                value_rows[row_start:row_stop],
                cache_len[request],
                block_table[request],
                k_pool,
                v_pool,
            )
        )
    return jnp.concatenate(outputs, axis=0)


PAGES_STEP = 16
LANES = 128


def flash_kernel(
    lens_ref, table_ref, q_ref, kn_ref, vn_ref, key_hbm, value_hbm, out_ref,
    key_buf, value_buf, copy_sem, top_sc, sum_sc, acc_sc,
):
    request = pl.program_id(0)
    length = lens_ref[request]
    rows = q_ref.shape[0]
    block_len = key_buf.shape[2]
    span = PAGES_STEP * block_len
    table_width = table_ref.shape[0] // pl.num_programs(0)
    blocks = (length + block_len - 1) // block_len
    turns = (length + span - 1) // span
    log2_scale = math.log2(math.e) / math.sqrt(HD)

    top_sc[...] = jnp.full(top_sc.shape, masked_score, jnp.float32)
    sum_sc[...] = jnp.zeros(sum_sc.shape, jnp.float32)
    acc_sc[...] = jnp.zeros(acc_sc.shape, jnp.float32)

    def page_copies(turn, slot):
        result = []
        for slot_page in range(PAGES_STEP):
            chosen = jnp.minimum(turn * PAGES_STEP + slot_page, jnp.maximum(blocks - 1, 0))
            page = table_ref[request * table_width + chosen]
            result.append(
                pltpu.make_async_copy(
                    key_hbm.at[page], key_buf.at[slot, slot_page], copy_sem.at[0, slot, slot_page]
                )
            )
            result.append(
                pltpu.make_async_copy(
                    value_hbm.at[page], value_buf.at[slot, slot_page], copy_sem.at[1, slot, slot_page]
                )
            )
        return result

    def absorb(keys, values, keep):
        for a in range(QPK):
            query = q_ref[:, a * HD : (a + 1) * HD]
            scores = (
                lax.dot_general(
                    query, keys, (((1,), (1,)), ((), ())), preferred_element_type=jnp.float32
                )
                * log2_scale
            )
            if keep is not None:
                scores = jnp.where(keep, scores, masked_score)
            running_top = top_sc[a]
            new_top = jnp.maximum(running_top, jnp.max(scores, axis=1, keepdims=True))
            weights = jnp.exp2(scores - new_top[:, :1])
            factor = jnp.exp2(running_top - new_top)
            sum_sc[a] = sum_sc[a] * factor + jnp.sum(weights, axis=1, keepdims=True)
            product = jnp.dot(
                weights.astype(jnp.bfloat16), values, preferred_element_type=jnp.float32
            )
            acc_sc[a] = acc_sc[a] * factor[:, :1] + product
            top_sc[a] = new_top

    @pl.when(turns > 0)
    def _():
        for copy in page_copies(0, 0):
            copy.start()

    def one_turn(turn, carried):
        slot = turn % 2

        @pl.when(turn + 1 < turns)
        def _():
            for copy in page_copies(turn + 1, 1 - slot):
                copy.start()

        for copy in page_copies(turn, slot):
            copy.wait()
        keys = key_buf[slot].reshape(span, HD)
        values = value_buf[slot].reshape(span, HD)
        whole = (turn + 1) * span <= length

        @pl.when(whole)
        def _():
            absorb(keys, values, None)

        @pl.when(jnp.logical_not(whole))
        def _():
            placed = turn * span + lax.broadcasted_iota(jnp.int32, (1, span), 1)
            absorb(keys, values, placed < length)

        return carried

    lax.fori_loop(0, turns, one_turn, 0)
    causal = lax.broadcasted_iota(jnp.int32, (rows, rows), 0) >= lax.broadcasted_iota(
        jnp.int32, (rows, rows), 1
    )
    absorb(kn_ref[...], vn_ref[...], causal)
    for a in range(QPK):
        out_ref[:, a * HD : (a + 1) * HD] = (acc_sc[a] / sum_sc[a][:, :1]).astype(out_ref.dtype)


def flash_attend(queries, key_rows, value_rows, cache_len, block_table, k_pool, v_pool):
    requests, table_width = block_table.shape
    pages_here, _, block_len, _ = k_pool.shape
    key_pages = k_pool.reshape(pages_here, block_len, HD)
    value_pages = v_pool.reshape(pages_here, block_len, HD)
    rows = queries.shape[0] // requests

    def row_spec(width):
        return pl.BlockSpec((rows, width), lambda request, lens_ref, table_ref: (request, 0))

    grid_spec = pltpu.PrefetchScalarGridSpec(
        num_scalar_prefetch=2,
        grid=(requests,),
        in_specs=[row_spec(QPK * HD), row_spec(HD), row_spec(HD)]
        + [pl.BlockSpec(memory_space=pl.ANY)] * 2,
        out_specs=row_spec(QPK * HD),
        scratch_shapes=[
            pltpu.VMEM((2, PAGES_STEP, block_len, HD), jnp.bfloat16),
            pltpu.VMEM((2, PAGES_STEP, block_len, HD), jnp.bfloat16),
            pltpu.SemaphoreType.DMA((2, 2, PAGES_STEP)),
            pltpu.VMEM((QPK, rows, LANES), jnp.float32),
            pltpu.VMEM((QPK, rows, LANES), jnp.float32),
            pltpu.VMEM((QPK, rows, HD), jnp.float32),
        ],
    )
    return pl.pallas_call(
        flash_kernel,
        grid_spec=grid_spec,
        out_shape=jax.ShapeDtypeStruct((queries.shape[0], QPK * HD), jnp.bfloat16),
        compiler_params=pltpu.CompilerParams(dimension_semantics=("arbitrary",)),
    )(cache_len, block_table.reshape(-1), queries, key_rows, value_rows, key_pages, value_pages)


def project_kernel(
    x_ref, g_ref, w_ref, cos_ref, sin_ref, qg_ref, kg_ref, q_out, k_out, v_out, n_out
):
    hidden = x_ref[...].astype(jnp.float32)
    mean_square = jnp.mean(hidden * hidden, axis=1, keepdims=True)
    normed_rows = (hidden * lax.rsqrt(mean_square + norm_eps) * g_ref[...]).astype(n_out.dtype)
    n_out[...] = normed_rows
    projected = jnp.dot(normed_rows, w_ref[...], preferred_element_type=jnp.float32)
    cosine = cos_ref[...]
    sine = sin_ref[...]

    def norm_rotate(part, gain):
        squares = jnp.mean(part * part, axis=1, keepdims=True)
        normed = part * lax.rsqrt(squares + norm_eps) * gain
        return normed * cosine + pltpu.roll(normed, HD // 2, 1) * sine

    for a in range(QPK):
        q_out[:, a * HD : (a + 1) * HD] = norm_rotate(
            projected[:, a * HD : (a + 1) * HD], qg_ref[...]
        ).astype(q_out.dtype)
    k_out[...] = norm_rotate(
        projected[:, QPK * HD : QPK * HD + HD], kg_ref[...]
    ).astype(k_out.dtype)
    v_out[...] = projected[:, QPK * HD + HD : QPK * HD + 2 * HD].astype(v_out.dtype)


def project_prepare(group_rows, norm_gain, attend_columns, positions, q_gain, k_gain):
    row_count, width = group_rows.shape
    half_width = HD // 2
    frequency = jnp.exp(
        jnp.arange(half_width, dtype=jnp.float32) * (-2.0 * math.log(rope_base) / HD)
    )
    angle = positions.astype(jnp.float32)[:, None] * frequency[None, :]
    cosine = jnp.cos(angle)
    sine_wave = jnp.sin(angle)
    cos_full = jnp.concatenate([cosine, cosine], axis=1)
    sin_signed = jnp.concatenate([-sine_wave, sine_wave], axis=1)
    block_rows = 256
    columns = attend_columns.shape[1]

    def rows_of(cols):
        return pl.BlockSpec((block_rows, cols), lambda i: (i, 0))

    whole = lambda shape: pl.BlockSpec(shape, lambda i: (0, 0))
    return pl.pallas_call(
        project_kernel,
        grid=(row_count // block_rows,),
        in_specs=[
            rows_of(width),
            whole((1, width)),
            whole((width, columns)),
            rows_of(HD),
            rows_of(HD),
            whole((1, HD)),
            whole((1, HD)),
        ],
        out_specs=[rows_of(QPK * HD), rows_of(HD), rows_of(HD), rows_of(width)],
        out_shape=[
            jax.ShapeDtypeStruct((row_count, QPK * HD), jnp.bfloat16),
            jax.ShapeDtypeStruct((row_count, HD), jnp.bfloat16),
            jax.ShapeDtypeStruct((row_count, HD), jnp.bfloat16),
            jax.ShapeDtypeStruct((row_count, width), jnp.bfloat16),
        ],
    )(group_rows, norm_gain.reshape(1, width), attend_columns, cos_full, sin_signed, q_gain.reshape(1, HD), k_gain.reshape(1, HD))


def lengths_of(row_ids, cache_len):
    owners = row_ids // NEW_TOK
    matches = owners[:, None] == jnp.arange(cache_len.shape[0], dtype=jnp.int32)[None, :]
    return jnp.sum(jnp.where(matches, cache_len[None, :], 0), axis=1) + row_ids % NEW_TOK


def add_rows(left_side, weight_piece):
    return jnp.dot(left_side, weight_piece, preferred_element_type=jnp.float32)


def gather_columns(piece):
    req_count = lax.axis_size("req")
    copies = jnp.broadcast_to(piece[None], (req_count,) + piece.shape)
    return lax.all_to_all(copies, "req", 0, 0, tiled=True).reshape(-1, piece.shape[1])


def on_device(hidden_in, norm_gain, q_gain, k_gain, w_proj, cache_len, block_table, k_pool, v_pool):
    split = QPK * HD + 2 * HD
    attend_columns = gather_columns(w_proj[:, :split])
    gate_columns = lax.all_gather(w_proj[:, split:], "req", axis=0, tiled=True)
    group_hidden = lax.all_gather(hidden_in, "head", axis=0, tiled=True)
    row_ids = jnp.arange(group_hidden.shape[0], dtype=jnp.int32)
    positions = lengths_of(row_ids, cache_len)
    queries, key_rows, value_rows, group_rows = project_prepare(
        group_hidden, norm_gain, attend_columns, positions, q_gain, k_gain
    )
    attention = flash_attend(
        queries, key_rows, value_rows, cache_len, block_table, k_pool, v_pool
    )
    gate_rows = add_rows(group_rows, gate_columns)
    gated = (attention.astype(jnp.float32) * jax.nn.sigmoid(gate_rows)).astype(jnp.bfloat16)
    return lax.all_to_all(gated, "head", split_axis=0, concat_axis=1, tiled=True)


def solution(mesh):
    in_specs = (
        P(("req", "head"), None),
        P(),
        P(),
        P(),
        P("req", "head"),
        P("req"),
        P("req", None),
        P("req", "head", None, None),
        P("req", "head", None, None),
    )
    out_specs = P(("req", "head"), None)
    return jax.shard_map(
        on_device, mesh=mesh, in_specs=in_specs, out_specs=out_specs, check_vma=False
    )
```

```python
import math

import jax
import jax.numpy as jnp
from jax import lax
from jax.experimental import pallas as pl
from jax.experimental.pallas import tpu as pltpu
from jax.sharding import PartitionSpec as P

KVH = 8
HD = 128
QPK = 2
NEW_TOK = 512


rope_base = 1000000.0
norm_eps = 1e-06
masked_score = -1e30


def row_norm(values, weight_gain):
    squares = jnp.mean(values * values, axis=-1, keepdims=True)
    return values * lax.rsqrt(squares + norm_eps) * weight_gain


def rotate(values, positions):
    half_width = values.shape[-1] // 2
    frequency = jnp.exp(
        jnp.arange(half_width, dtype=jnp.float32) * (-2.0 * math.log(rope_base) / values.shape[-1])
    )
    angle = positions.astype(jnp.float32)[:, None] * frequency[None, :]
    bcast_shape = (angle.shape[0],) + (1,) * (values.ndim - 2) + (half_width,)
    cosine = jnp.cos(angle).reshape(bcast_shape)
    sine_wave = jnp.sin(angle).reshape(bcast_shape)
    first_half = values[..., :half_width]
    second_half = values[..., half_width:]
    return jnp.concatenate(
        [
            first_half * cosine - second_half * sine_wave,
            second_half * cosine + first_half * sine_wave,
        ],
        axis=-1,
    )


def prepare(projected, positions, q_gain, k_gain):
    row_count = projected.shape[0]
    queries = projected[:, : QPK * HD].reshape(row_count, QPK, HD)
    key_part = projected[:, QPK * HD : QPK * HD + HD]
    value_part = projected[:, QPK * HD + HD : QPK * HD + 2 * HD]
    queries = (
        rotate(row_norm(queries, q_gain), positions)
        .astype(jnp.bfloat16)
        .reshape(row_count, QPK * HD)
    )
    key_part = rotate(row_norm(key_part, k_gain), positions).astype(jnp.bfloat16)
    value_part = value_part.astype(jnp.bfloat16)
    return (queries, key_part, value_part)


def update(carried, scores, values):
    running_top, running_sum, running_acc = carried
    new_top = jnp.maximum(running_top, jnp.max(scores, axis=-1))
    weights = jnp.exp(scores - new_top[..., None])
    factor = jnp.exp(running_top - new_top)
    new_sum = running_sum * factor + jnp.sum(weights, axis=-1)
    product = jnp.einsum(
        "hrs,hsd->hrd", weights.astype(jnp.bfloat16), values, preferred_element_type=jnp.float32
    )
    return (new_top, new_sum, running_acc * factor[..., None] + product)


def attend_one(queries, key_new, value_new, length, pages, k_pool, v_pool):
    heads_here = k_pool.shape[1]
    block_len = k_pool.shape[2]
    new_count = key_new.shape[0]
    row_total = new_count * QPK
    query_rows = (
        queries.reshape(new_count, heads_here, QPK, HD)
        .transpose(1, 0, 2, 3)
        .reshape(heads_here, row_total, HD)
    )
    step_pages = min(pages.shape[0], max(1, 1024 // block_len))
    span_keys = step_pages * block_len
    scale_factor = 1.0 / math.sqrt(HD)

    def one_turn(turn_index, carried):
        chosen = lax.dynamic_slice_in_dim(pages, turn_index * step_pages, step_pages)
        key_block = k_pool[chosen].transpose(1, 0, 2, 3).reshape(heads_here, span_keys, HD)
        value_block = v_pool[chosen].transpose(1, 0, 2, 3).reshape(heads_here, span_keys, HD)
        scores = (
            jnp.einsum("hrd,hsd->hrs", query_rows, key_block, preferred_element_type=jnp.float32)
            * scale_factor
        )
        placed = turn_index * span_keys + jnp.arange(span_keys, dtype=jnp.int32)
        scores = jnp.where(placed[None, None, :] < length, scores, masked_score)
        return update(carried, scores, value_block)

    start_state = (
        jnp.full((heads_here, row_total), masked_score, jnp.float32),
        jnp.zeros((heads_here, row_total), jnp.float32),
        jnp.zeros((heads_here, row_total, HD), jnp.float32),
    )
    turn_count = (length + span_keys - 1) // span_keys
    carried = lax.fori_loop(jnp.int32(0), turn_count, one_turn, start_state)
    new_keys = key_new.reshape(new_count, heads_here, HD).transpose(1, 0, 2)
    new_values = value_new.reshape(new_count, heads_here, HD).transpose(1, 0, 2)
    scores = (
        jnp.einsum("hrd,hsd->hrs", query_rows, new_keys, preferred_element_type=jnp.float32)
        * scale_factor
    )
    causal = (
        jnp.arange(row_total, dtype=jnp.int32)[:, None] // QPK
        >= jnp.arange(new_count, dtype=jnp.int32)[None, :]
    )
    scores = jnp.where(causal[None], scores, masked_score)
    top_row, sum_row, acc_row = update(carried, scores, new_values)
    result = acc_row / sum_row[..., None]
    return (
        result.reshape(heads_here, new_count, QPK, HD)
        .transpose(1, 0, 2, 3)
        .reshape(new_count, heads_here * QPK * HD)
    )


def attend_group(queries, key_rows, value_rows, cache_len, block_table, k_pool, v_pool):
    outputs = []
    for request in range(cache_len.shape[0]):
        row_start = request * NEW_TOK
        row_stop = row_start + NEW_TOK
        outputs.append(
            attend_one(
                queries[row_start:row_stop],
                key_rows[row_start:row_stop],
                value_rows[row_start:row_stop],
                cache_len[request],
                block_table[request],
                k_pool,
                v_pool,
            )
        )
    return jnp.concatenate(outputs, axis=0)


PAGES_STEP = 16
LANES = 128


def flash_kernel(
    lens_ref, table_ref, q_ref, kn_ref, vn_ref, key_hbm, value_hbm, out_ref,
    key_buf, value_buf, copy_sem, top_sc, sum_sc, acc_sc,
):
    request = pl.program_id(0)
    length = lens_ref[request]
    rows = q_ref.shape[0]
    block_len = key_buf.shape[2]
    span = PAGES_STEP * block_len
    table_width = table_ref.shape[0] // pl.num_programs(0)
    blocks = (length + block_len - 1) // block_len
    turns = (length + span - 1) // span
    log2_scale = math.log2(math.e) / math.sqrt(HD)

    top_sc[...] = jnp.full(top_sc.shape, masked_score, jnp.float32)
    sum_sc[...] = jnp.zeros(sum_sc.shape, jnp.float32)
    acc_sc[...] = jnp.zeros(acc_sc.shape, jnp.float32)

    def page_copies(turn, slot, owner=None, owner_blocks=None):
        if owner is None:
            owner, owner_blocks = request, blocks
        result = []
        for slot_page in range(PAGES_STEP):
            chosen = jnp.minimum(turn * PAGES_STEP + slot_page, jnp.maximum(owner_blocks - 1, 0))
            page = table_ref[owner * table_width + chosen]
            result.append(
                pltpu.make_async_copy(
                    key_hbm.at[page], key_buf.at[slot, slot_page], copy_sem.at[0, slot, slot_page]
                )
            )
            result.append(
                pltpu.make_async_copy(
                    value_hbm.at[page], value_buf.at[slot, slot_page], copy_sem.at[1, slot, slot_page]
                )
            )
        return result

    def absorb(keys, values, keep):
        for a in range(QPK):
            query = q_ref[:, a * HD : (a + 1) * HD]
            scores = (
                lax.dot_general(
                    query, keys, (((1,), (1,)), ((), ())), preferred_element_type=jnp.float32
                )
                * log2_scale
            )
            if keep is not None:
                scores = jnp.where(keep, scores, masked_score)
            running_top = top_sc[a]
            new_top = jnp.maximum(running_top, jnp.max(scores, axis=1, keepdims=True))
            weights = jnp.exp2(scores - new_top[:, :1])
            factor = jnp.exp2(running_top - new_top)
            sum_sc[a] = sum_sc[a] * factor + jnp.sum(weights, axis=1, keepdims=True)
            product = jnp.dot(
                weights.astype(jnp.bfloat16), values, preferred_element_type=jnp.float32
            )
            acc_sc[a] = acc_sc[a] * factor[:, :1] + product
            top_sc[a] = new_top

    @pl.when(jnp.logical_and(request == 0, turns > 0))
    def _():
        for copy in page_copies(0, 0):
            copy.start()

    def one_turn(turn, carried):
        slot = turn % 2

        @pl.when(turn + 1 < turns)
        def _():
            for copy in page_copies(turn + 1, 1 - slot):
                copy.start()

        for copy in page_copies(turn, slot):
            copy.wait()
        keys = key_buf[slot].reshape(span, HD)
        values = value_buf[slot].reshape(span, HD)
        whole = (turn + 1) * span <= length

        @pl.when(whole)
        def _():
            absorb(keys, values, None)

        @pl.when(jnp.logical_not(whole))
        def _():
            placed = turn * span + lax.broadcasted_iota(jnp.int32, (1, span), 1)
            absorb(keys, values, placed < length)

        return carried

    lax.fori_loop(0, turns, one_turn, 0)
    following = request + 1
    following_len = lens_ref[jnp.minimum(following, pl.num_programs(0) - 1)]
    following_blocks = (following_len + block_len - 1) // block_len

    @pl.when(jnp.logical_and(following < pl.num_programs(0), following_len > 0))
    def _():
        for copy in page_copies(0, 0, following, following_blocks):
            copy.start()
    causal = lax.broadcasted_iota(jnp.int32, (rows, rows), 0) >= lax.broadcasted_iota(
        jnp.int32, (rows, rows), 1
    )
    absorb(kn_ref[...], vn_ref[...], causal)
    for a in range(QPK):
        out_ref[:, a * HD : (a + 1) * HD] = (acc_sc[a] / sum_sc[a][:, :1]).astype(out_ref.dtype)


def flash_attend(queries, key_rows, value_rows, cache_len, block_table, k_pool, v_pool):
    requests, table_width = block_table.shape
    pages_here, _, block_len, _ = k_pool.shape
    key_pages = k_pool.reshape(pages_here, block_len, HD)
    value_pages = v_pool.reshape(pages_here, block_len, HD)
    rows = queries.shape[0] // requests

    def row_spec(width):
        return pl.BlockSpec((rows, width), lambda request, lens_ref, table_ref: (request, 0))

    grid_spec = pltpu.PrefetchScalarGridSpec(
        num_scalar_prefetch=2,
        grid=(requests,),
        in_specs=[row_spec(QPK * HD), row_spec(HD), row_spec(HD)]
        + [pl.BlockSpec(memory_space=pl.ANY)] * 2,
        out_specs=row_spec(QPK * HD),
        scratch_shapes=[
            pltpu.VMEM((2, PAGES_STEP, block_len, HD), jnp.bfloat16),
            pltpu.VMEM((2, PAGES_STEP, block_len, HD), jnp.bfloat16),
            pltpu.SemaphoreType.DMA((2, 2, PAGES_STEP)),
            pltpu.VMEM((QPK, rows, LANES), jnp.float32),
            pltpu.VMEM((QPK, rows, LANES), jnp.float32),
            pltpu.VMEM((QPK, rows, HD), jnp.float32),
        ],
    )
    return pl.pallas_call(
        flash_kernel,
        grid_spec=grid_spec,
        out_shape=jax.ShapeDtypeStruct((queries.shape[0], QPK * HD), jnp.bfloat16),
        compiler_params=pltpu.CompilerParams(dimension_semantics=("arbitrary",)),
    )(cache_len, block_table.reshape(-1), queries, key_rows, value_rows, key_pages, value_pages)


def project_kernel(
    x_ref, g_ref, w_ref, cos_ref, sin_ref, qg_ref, kg_ref, q_out, k_out, v_out, n_out
):
    hidden = x_ref[...].astype(jnp.float32)
    mean_square = jnp.mean(hidden * hidden, axis=1, keepdims=True)
    normed_rows = (hidden * lax.rsqrt(mean_square + norm_eps) * g_ref[...]).astype(n_out.dtype)
    n_out[...] = normed_rows
    projected = jnp.dot(normed_rows, w_ref[...], preferred_element_type=jnp.float32)
    cosine = cos_ref[...]
    sine = sin_ref[...]

    def norm_rotate(part, gain):
        squares = jnp.mean(part * part, axis=1, keepdims=True)
        normed = part * lax.rsqrt(squares + norm_eps) * gain
        return normed * cosine + pltpu.roll(normed, HD // 2, 1) * sine

    for a in range(QPK):
        q_out[:, a * HD : (a + 1) * HD] = norm_rotate(
            projected[:, a * HD : (a + 1) * HD], qg_ref[...]
        ).astype(q_out.dtype)
    k_out[...] = norm_rotate(
        projected[:, QPK * HD : QPK * HD + HD], kg_ref[...]
    ).astype(k_out.dtype)
    v_out[...] = projected[:, QPK * HD + HD : QPK * HD + 2 * HD].astype(v_out.dtype)


def project_prepare(group_rows, norm_gain, attend_columns, positions, q_gain, k_gain):
    row_count, width = group_rows.shape
    half_width = HD // 2
    frequency = jnp.exp(
        jnp.arange(half_width, dtype=jnp.float32) * (-2.0 * math.log(rope_base) / HD)
    )
    angle = positions.astype(jnp.float32)[:, None] * frequency[None, :]
    cosine = jnp.cos(angle)
    sine_wave = jnp.sin(angle)
    cos_full = jnp.concatenate([cosine, cosine], axis=1)
    sin_signed = jnp.concatenate([-sine_wave, sine_wave], axis=1)
    block_rows = 256
    columns = attend_columns.shape[1]

    def rows_of(cols):
        return pl.BlockSpec((block_rows, cols), lambda i: (i, 0))

    whole = lambda shape: pl.BlockSpec(shape, lambda i: (0, 0))
    return pl.pallas_call(
        project_kernel,
        grid=(row_count // block_rows,),
        in_specs=[
            rows_of(width),
            whole((1, width)),
            whole((width, columns)),
            rows_of(HD),
            rows_of(HD),
            whole((1, HD)),
            whole((1, HD)),
        ],
        out_specs=[rows_of(QPK * HD), rows_of(HD), rows_of(HD), rows_of(width)],
        out_shape=[
            jax.ShapeDtypeStruct((row_count, QPK * HD), jnp.bfloat16),
            jax.ShapeDtypeStruct((row_count, HD), jnp.bfloat16),
            jax.ShapeDtypeStruct((row_count, HD), jnp.bfloat16),
            jax.ShapeDtypeStruct((row_count, width), jnp.bfloat16),
        ],
    )(group_rows, norm_gain.reshape(1, width), attend_columns, cos_full, sin_signed, q_gain.reshape(1, HD), k_gain.reshape(1, HD))


def lengths_of(row_ids, cache_len):
    owners = row_ids // NEW_TOK
    matches = owners[:, None] == jnp.arange(cache_len.shape[0], dtype=jnp.int32)[None, :]
    return jnp.sum(jnp.where(matches, cache_len[None, :], 0), axis=1) + row_ids % NEW_TOK


def add_rows(left_side, weight_piece):
    return jnp.dot(left_side, weight_piece, preferred_element_type=jnp.float32)


def gather_columns(piece):
    req_count = lax.axis_size("req")
    copies = jnp.broadcast_to(piece[None], (req_count,) + piece.shape)
    return lax.all_to_all(copies, "req", 0, 0, tiled=True).reshape(-1, piece.shape[1])


def on_device(hidden_in, norm_gain, q_gain, k_gain, w_proj, cache_len, block_table, k_pool, v_pool):
    split = QPK * HD + 2 * HD
    attend_columns = gather_columns(w_proj[:, :split])
    gate_columns = lax.all_gather(w_proj[:, split:], "req", axis=0, tiled=True)
    group_hidden = lax.all_gather(hidden_in, "head", axis=0, tiled=True)
    row_ids = jnp.arange(group_hidden.shape[0], dtype=jnp.int32)
    positions = lengths_of(row_ids, cache_len)
    queries, key_rows, value_rows, group_rows = project_prepare(
        group_hidden, norm_gain, attend_columns, positions, q_gain, k_gain
    )
    attention = flash_attend(
        queries, key_rows, value_rows, cache_len, block_table, k_pool, v_pool
    )
    gate_rows = add_rows(group_rows, gate_columns)
    gated = (attention.astype(jnp.float32) * jax.nn.sigmoid(gate_rows)).astype(jnp.bfloat16)
    return lax.all_to_all(gated, "head", split_axis=0, concat_axis=1, tiled=True)


def solution(mesh):
    in_specs = (
        P(("req", "head"), None),
        P(),
        P(),
        P(),
        P("req", "head"),
        P("req"),
        P("req", None),
        P("req", "head", None, None),
        P("req", "head", None, None),
    )
    out_specs = P(("req", "head"), None)
    return jax.shard_map(
        on_device, mesh=mesh, in_specs=in_specs, out_specs=out_specs, check_vma=False
    )
```
